128 devices in a mesh: nodes: 128 (over x, z, y, core).
Axes of the slice: x: 4, y: 4, z: 4, core: 2. Of those that a mesh axis runs over, the one named last changes fastest.
Arguments:
- features: bfloat16 [1048576, 256], P('nodes'), may hold values from -6 to 6
- cluster_ids: int32 [1048576], P('nodes'), may hold values from 0 to 65535, as said below
- tile_cols: int32 [512, 6], P('nodes'), may hold values from 0 to 511, as said below
- tile_counts: int32 [512], P('nodes'), may hold values from 1 to 6
- adjacency: bfloat16 [512, 6, 128, 128], P('nodes'), may hold values from -0.5 to 0.5
- w_first: bfloat16 [256, 256], replicated, may hold values from -0.375 to 0.375
- w_second: bfloat16 [256, 256], replicated, may hold values from -0.375 to 0.375
Outputs:
- unpooled: bfloat16 [1048576, 256], P('nodes')
The draws below stay inside these ranges and needn't reach their ends.
Inputs may be any that keep to these rules, and one draw needn't show every extreme that they name: `cluster_ids`: cluster c is held by device c // 512. Exactly 1024 fine nodes of each device name clusters of other devices; at most 16 of them name clusters of any one other device, among at most 4 distinct clusters of it. `tile_cols`: tile s holds clusters s * 128 to s * 128 + 127; the column tiles named for a tile row of device p are tiles of devices p - 1, p and p + 1.
All inputs are finite; a program needn't handle non-finite values.
Results may differ from the reference program's by a relative error of at most 0.0051.
Values may be sent and summed in bfloat16 or wider, within the bound.
No kernel may reach another device: no remote copies, remote signals or barrier semaphores. Data moves between devices by JAX's collectives and lax.ppermute only.
A program may use at most 64 MiB of HBM per device.

```python
import jax
import jax.numpy as jnp
from jax import lax

F = 256
FINE_DEV = 8192
CL_DEV = 512
TILE = 128
KT = 6
CAP = 16
DCAP = 4
BND = 1024
NFINE = 1048576
NCLUS = 65536
TILES_DEV = 4
NTILES = 512
N_NODES = 128


def draw_cluster_ids(key, part):
    key_star, key_devices = jax.random.split(jax.random.fold_in(key, 11))
    target = jax.random.randint(key_star, (), 0, N_NODES)
    device_keys = jax.random.split(key_devices, N_NODES)
    devices = jnp.arange(N_NODES, dtype=jnp.int32)

    def one_device(dev_key, device):
        key_a, key_b, key_c, key_d, key_e = jax.random.split(dev_key, 5)
        filled = jnp.where(device == target, (target + 1) % N_NODES, target)
        positions = (N_NODES - 1) * CAP
        spots = jnp.arange(positions, dtype=jnp.int32)
        owner_of = (device + 1 + spots // CAP) % N_NODES
        slot_of = spots % CAP
        ranking = jax.random.permutation(key_a, positions).astype(jnp.int32)
        scores = jnp.where(owner_of == filled, ranking - positions, ranking)
        picked = jnp.argsort(scores, stable=True)[:BND]
        picked_owner = owner_of[picked]
        picked_slot = slot_of[picked]
        bases = jax.random.randint(key_b, (N_NODES,), 0, CL_DEV)
        extra = jax.random.randint(key_c, (BND,), 0, DCAP)
        member = jnp.where(picked_slot < DCAP, picked_slot, extra)
        within = (bases[picked_owner] + member * (CL_DEV // DCAP)) % CL_DEV
        boundary_ids = picked_owner * CL_DEV + within
        interior = device * CL_DEV + jax.random.randint(key_d, (FINE_DEV,), 0, CL_DEV)
        places = jax.random.permutation(key_e, FINE_DEV)[:BND]
        return interior.at[places].set(boundary_ids)
    result = jax.vmap(one_device)(device_keys, devices)
    return result.reshape(-1).astype(jnp.int32)


def draw_tile_cols(key, part):
    sub_key = jax.random.fold_in(key, 21)
    tile_ids = jnp.arange(NTILES, dtype=jnp.int32)
    holder = tile_ids // TILES_DEV
    lowest = jnp.maximum(holder - 1, 0) * TILES_DEV
    highest = jnp.minimum(holder + 2, N_NODES) * TILES_DEV
    raw_ints = jax.random.randint(sub_key, (NTILES, KT), 0, 1 << 20)
    columns = lowest[:, None] + raw_ints % (highest - lowest)[:, None]
    columns = columns.at[:, 0].set(tile_ids)
    return columns.astype(jnp.int32)


def draw_tile_counts(key, part):
    key_a, key_b = jax.random.split(jax.random.fold_in(key, 31))
    counts = jax.random.randint(key_a, (NTILES,), 1, KT + 1)
    fullest = jax.random.randint(key_b, (), 0, NTILES)
    counts = counts.at[fullest].set(KT)
    return counts.astype(jnp.int32)


def steps_of(rng, shape, cuts, least, high):
    def one(axis_at, blocks):
        heights = jax.random.uniform(jax.random.fold_in(jax.random.fold_in(rng, 6), axis_at), (blocks,), jnp.float32, least / len(cuts), high / len(cuts))
        return jnp.repeat(jnp.exp(heights), shape[axis_at] // blocks).reshape((-1,) + (1,) * (len(shape) - axis_at - 1))

    loudness = one(*cuts[0])
    for cut in cuts[1:]:
        loudness = loudness * one(*cut)
    return loudness


def scatter_about(stream_key, shape, spread, reach, cuts=(), kind=jnp.bfloat16):
    values = jax.random.normal(stream_key, shape, jnp.float32) * spread
    if len(cuts) > 0:
        values = steps_of(stream_key, shape, cuts, -0.22, 0.18) * values
    return jnp.clip(values, min=-reach, max=reach).astype(kind)


def setup_inputs(seed: int = 0) -> dict:
    key_list = jax.random.split(jax.random.key(seed), 8)
    return {
        "features": scatter_about(key_list[0], (NFINE, F), 1.0, 6.0, ((0, 128),)),
        "cluster_ids": draw_cluster_ids(jax.random.fold_in(key_list[7], 71), 0),
        "tile_cols": draw_tile_cols(jax.random.fold_in(key_list[7], 71), 0),
        "tile_counts": draw_tile_counts(jax.random.fold_in(key_list[7], 71), 0),
        "adjacency": scatter_about(key_list[4], (NTILES, KT, TILE, TILE), ((TILE * KT) ** -0.5), 0.5, ((0, 128),)),
        "w_first": scatter_about(key_list[5], (F, F), F ** -0.5, 0.375),
        "w_second": scatter_about(key_list[6], (F, F), F ** -0.5, 0.375),
    }


def convolve(values, tile_cols, tile_counts, adjacency):
    tiles = values.reshape(NTILES, TILE, F)
    live = (jnp.arange(KT, dtype=jnp.int32)[None, :] < tile_counts[:, None]).astype(jnp.float32)

    def one_tile(pieces):
        weights, cols, keep = pieces
        picked = tiles[cols].astype(jnp.float32)
        scaled = weights.astype(jnp.float32) * keep[:, None, None]
        return jnp.einsum('kij,kjf->if', scaled, picked)
    result = lax.map(one_tile, (adjacency, tile_cols, live))
    return result.reshape(NCLUS, F)

def reference(features, cluster_ids, tile_cols, tile_counts, adjacency, w_first, w_second):
    feature_blocks = features.reshape(N_NODES, FINE_DEV, F)
    id_blocks = cluster_ids.reshape(N_NODES, FINE_DEV)

    def add_block(running, pieces):
        sums_acc, counts_acc = running
        rows_x, ids_x = pieces
        sums_acc = sums_acc.at[ids_x].add(rows_x.astype(jnp.float32))
        counts_acc = counts_acc.at[ids_x].add(jnp.ones((FINE_DEV,), jnp.float32))
        return ((sums_acc, counts_acc), None)
    start = (jnp.zeros((NCLUS, F), jnp.float32), jnp.zeros((NCLUS,), jnp.float32))
    (sums_all, counts_all), _ = lax.scan(add_block, start, (feature_blocks, id_blocks))
    pooled = (sums_all / jnp.sqrt(counts_all + 1.0)[:, None]).astype(jnp.bfloat16)
    first_proj = jnp.dot(pooled, w_first, preferred_element_type=jnp.float32).astype(jnp.bfloat16)
    hidden = jnp.maximum(convolve(first_proj, tile_cols, tile_counts, adjacency), 0.0).astype(jnp.bfloat16)
    second_proj = jnp.dot(hidden, w_second, preferred_element_type=jnp.float32).astype(jnp.bfloat16)
    coarse = convolve(second_proj, tile_cols, tile_counts, adjacency).astype(jnp.bfloat16)

    def unpool_block(pieces):
        rows_x, ids_x = pieces
        return (rows_x.astype(jnp.float32) + coarse[ids_x].astype(jnp.float32)).astype(jnp.bfloat16)
    result = lax.map(unpool_block, (feature_blocks, id_blocks))
    return result.reshape(NFINE, F)
```

```python
import jax
import jax.numpy as jnp
from jax import lax
from jax.sharding import PartitionSpec as P

DCAP = 4


def with_halo(block, sides, width):
    for axis, dim in sides:
        count = lax.axis_size(axis)
        forward = [(i, i + 1) for i in range(count - 1)]
        backward = [(target, source) for source, target in forward]
        low = lax.ppermute(
            lax.slice_in_dim(block, block.shape[dim] - width, None, axis=dim), axis, forward
        )
        high = lax.ppermute(lax.slice_in_dim(block, 0, width, axis=dim), axis, backward)
        block = jnp.concatenate([low, block, high], axis=dim)
    return block


def convolve(values, tile_cols, tile_counts, adjacency, myself):
    window = with_halo(values, (("nodes", 0),), values.shape[0])
    tile_size = adjacency.shape[2]
    per_device = tile_cols.shape[0]
    window_tiles = window.reshape(-1, tile_size, window.shape[1])
    offsets = tile_cols - (myself - 1) * per_device
    picked = window_tiles[offsets]
    live = jnp.arange(tile_cols.shape[1], dtype=jnp.int32)[None, :] < tile_counts[:, None]
    weights = jnp.where(live[:, :, None, None], adjacency, jnp.zeros((), adjacency.dtype))
    result = jnp.einsum("tkij,tkjf->tif", weights, picked, preferred_element_type=jnp.float32)
    return result.reshape(values.shape[0], values.shape[1])


def distinct_slots(cluster_ids, owners, remote, device_count):
    peers = jnp.arange(device_count, dtype=jnp.int32)
    big = jnp.int32(2**30)
    owner_hot = (owners[:, None] == peers[None, :]) & remote[:, None]
    grid = jnp.where(owner_hot, cluster_ids[:, None], big)
    lows = []
    for _ in range(DCAP):
        low = jnp.min(grid, axis=0)
        lows.append(low)
        grid = jnp.where(grid > low[None, :], grid, big)
    rank = jnp.zeros(grid.shape, jnp.int32)
    for low in lows[1:]:
        rank = rank + (cluster_ids[:, None] >= low[None, :]).astype(jnp.int32)
    slot = jnp.sum(jnp.where(owner_hot, rank, 0), axis=1)
    return slot, jnp.stack(lows, axis=1)


def local(features, cluster_ids, tile_cols, tile_counts, adjacency, w_first, w_second):
    device_count = lax.axis_size("nodes")
    myself = lax.axis_index("nodes")
    fine_rows, width = features.shape
    clusters_here = adjacency.shape[0] * adjacency.shape[2]
    owners = cluster_ids // clusters_here
    remote = owners != myself
    slot, lows = distinct_slots(cluster_ids, owners, remote, device_count)
    remote_slots = device_count * DCAP
    column = jnp.where(
        remote, clusters_here + owners * DCAP + slot, cluster_ids - myself * clusters_here
    )
    columns = jnp.arange(clusters_here + remote_slots, dtype=jnp.int32)
    one_hot = (column[:, None] == columns[None, :]).astype(jnp.bfloat16)
    contract_rows = (((0,), (0,)), ((), ()))
    sums_ext = lax.dot_general(
        one_hot, features, contract_rows, preferred_element_type=jnp.float32
    )
    counts_ext = jnp.sum(one_hot.astype(jnp.float32), axis=0)

    dest_ids = jnp.where(lows < 2**30, lows - jnp.arange(device_count)[:, None] * clusters_here, -1)
    meta = jnp.zeros((remote_slots, 128), jnp.float32)
    meta = meta.at[:, 0].set(counts_ext[clusters_here:])
    meta = meta.at[:, 1].set(dest_ids.reshape(-1).astype(jnp.float32))
    payload = jnp.concatenate([sums_ext[clusters_here:], meta], axis=1)
    got = lax.all_to_all(
        payload.reshape(device_count, DCAP, -1), "nodes", split_axis=0, concat_axis=0, tiled=True
    ).reshape(remote_slots, -1)
    got_ids = got[:, width + 1].astype(jnp.int32)
    here = jnp.arange(clusters_here, dtype=jnp.int32)
    got_hot = (got_ids[:, None] == here[None, :]).astype(jnp.float32)
    sums_all = sums_ext[:clusters_here] + lax.dot_general(
        got_hot, got[:, :width], contract_rows,
        precision=lax.Precision.HIGHEST, preferred_element_type=jnp.float32,
    )
    counts_all = counts_ext[:clusters_here] + jnp.sum(got_hot * got[:, width:width + 1], axis=0)
    pooled = (sums_all / jnp.sqrt(counts_all + 1.0)[:, None]).astype(jnp.bfloat16)
    first_proj = jnp.dot(pooled, w_first, preferred_element_type=jnp.float32).astype(jnp.bfloat16)
    hidden = jnp.maximum(
        convolve(first_proj, tile_cols, tile_counts, adjacency, myself), 0.0
    ).astype(jnp.bfloat16)
    second_proj = jnp.dot(hidden, w_second, preferred_element_type=jnp.float32).astype(jnp.bfloat16)
    coarse = convolve(second_proj, tile_cols, tile_counts, adjacency, myself).astype(jnp.bfloat16)
    answers = jnp.dot(
        got_hot.astype(jnp.bfloat16), coarse, preferred_element_type=jnp.float32
    ).astype(jnp.bfloat16)
    returned = lax.all_to_all(
        answers.reshape(device_count, DCAP, width), "nodes", split_axis=0, concat_axis=0, tiled=True
    ).reshape(remote_slots, width)
    table = jnp.concatenate([coarse, returned], axis=0)
    value = features.astype(jnp.float32) + jnp.dot(
        one_hot, table, preferred_element_type=jnp.float32
    )
    return value.astype(jnp.bfloat16)


def solution(mesh):
    placed = (
        P("nodes", None),
        P("nodes"),
        P("nodes", None),
        P("nodes"),
        P("nodes", None, None, None),
        P(),
        P(),
    )
    return jax.shard_map(
        local, mesh=mesh, in_specs=placed, out_specs=P("nodes", None), check_vma=False
    )
```

```python
import jax
import jax.numpy as jnp
from jax import lax
from jax.sharding import PartitionSpec as P

DCAP = 4


def with_halo(block, sides, width):
    for axis, dim in sides:
        count = lax.axis_size(axis)
        forward = [(i, i + 1) for i in range(count - 1)]
        backward = [(target, source) for source, target in forward]
        low = lax.ppermute(
            lax.slice_in_dim(block, block.shape[dim] - width, None, axis=dim), axis, forward
        )
        high = lax.ppermute(lax.slice_in_dim(block, 0, width, axis=dim), axis, backward)
        block = jnp.concatenate([low, block, high], axis=dim)
    return block


def convolve(values, tile_cols, tile_counts, adjacency, myself):
    window = with_halo(values, (("nodes", 0),), values.shape[0])
    tile_size = adjacency.shape[2]
    per_device = tile_cols.shape[0]
    window_tiles = window.reshape(-1, tile_size, window.shape[1])
    offsets = tile_cols - (myself - 1) * per_device
    picked = window_tiles[offsets]
    live = jnp.arange(tile_cols.shape[1], dtype=jnp.int32)[None, :] < tile_counts[:, None]
    weights = jnp.where(live[:, :, None, None], adjacency, jnp.zeros((), adjacency.dtype))
    result = jnp.einsum("tkij,tkjf->tif", weights, picked, preferred_element_type=jnp.float32)
    return result.reshape(values.shape[0], values.shape[1])


def distinct_slots(owner_hot, lid_hot, clusters_here):
    contract_rows = (((0,), (0,)), ((), ()))
    presence = lax.dot_general(owner_hot, lid_hot, contract_rows, preferred_element_type=jnp.float32)
    named = (presence > 0).astype(jnp.bfloat16)
    lanes = jnp.arange(clusters_here, dtype=jnp.int32)
    before = (lanes[:, None] < lanes[None, :]).astype(jnp.bfloat16)
    rank = jnp.dot(named, before, preferred_element_type=jnp.float32)
    per_owner = jnp.dot(lid_hot, rank.T.astype(jnp.bfloat16), preferred_element_type=jnp.float32)
    slot = jnp.sum(per_owner * owner_hot.astype(jnp.float32), axis=1).astype(jnp.int32)
    return presence, rank, slot


def local(features, cluster_ids, tile_cols, tile_counts, adjacency, w_first, w_second):
    device_count = lax.axis_size("nodes")
    myself = lax.axis_index("nodes")
    fine_rows, width = features.shape
    clusters_here = adjacency.shape[0] * adjacency.shape[2]
    owners = cluster_ids // clusters_here
    lids = cluster_ids - owners * clusters_here
    remote = owners != myself
    peers = jnp.arange(device_count, dtype=jnp.int32)
    here = jnp.arange(clusters_here, dtype=jnp.int32)
    owner_hot = (owners[:, None] == peers[None, :]).astype(jnp.bfloat16)
    lid_hot = (lids[:, None] == here[None, :]).astype(jnp.bfloat16)
    presence, rank, slot = distinct_slots(owner_hot, lid_hot, clusters_here)
    remote_slots = device_count * DCAP
    slot_column = jnp.where(remote, owners * DCAP + slot, -1)
    slot_range = jnp.arange(remote_slots, dtype=jnp.int32)
    remote_hot = (slot_column[:, None] == slot_range[None, :]).astype(jnp.bfloat16)
    local_hot = jnp.where(remote[:, None], jnp.zeros((), jnp.bfloat16), lid_hot)
    contract_rows = (((0,), (0,)), ((), ()))
    remote_sums = lax.dot_general(
        remote_hot, features, contract_rows, preferred_element_type=jnp.float32
    )

    named = (presence > 0) & (peers != myself)[:, None]
    slot_counts = []
    slot_ids = []
    for k in range(DCAP):
        chosen = named & (rank == k)
        slot_counts.append(jnp.sum(jnp.where(chosen, presence, 0.0), axis=1))
        slot_ids.append(jnp.sum(jnp.where(chosen, here[None, :], 0), axis=1))
    slot_counts = jnp.stack(slot_counts, axis=1).reshape(-1)
    slot_ids = jnp.stack(slot_ids, axis=1).reshape(-1)
    meta_lanes = jnp.arange(128, dtype=jnp.int32)[None, :]
    meta = jnp.where(
        meta_lanes == 0,
        slot_counts[:, None],
        jnp.where(meta_lanes == 1, slot_ids[:, None].astype(jnp.float32), 0.0),
    )
    payload = jnp.concatenate([remote_sums, meta], axis=1)
    got = lax.all_to_all(
        payload.reshape(device_count, DCAP, -1), "nodes", split_axis=0, concat_axis=0, tiled=True
    ).reshape(remote_slots, -1)
    local_sums = lax.dot_general(
        local_hot, features, contract_rows, preferred_element_type=jnp.float32
    )
    local_counts = lax.dynamic_index_in_dim(presence, myself, axis=0, keepdims=False)
    got_ids = got[:, width + 1].astype(jnp.int32)
    got_hot = (got_ids[:, None] == here[None, :]).astype(jnp.float32)
    sums_all = local_sums + lax.dot_general(
        got_hot, got[:, :width], contract_rows,
        precision=lax.Precision.HIGHEST, preferred_element_type=jnp.float32,
    )
    counts_all = local_counts + jnp.sum(got_hot * got[:, width:width + 1], axis=0)
    pooled = (sums_all / jnp.sqrt(counts_all + 1.0)[:, None]).astype(jnp.bfloat16)
    first_proj = jnp.dot(pooled, w_first, preferred_element_type=jnp.float32).astype(jnp.bfloat16)
    hidden = jnp.maximum(
        convolve(first_proj, tile_cols, tile_counts, adjacency, myself), 0.0
    ).astype(jnp.bfloat16)
    second_proj = jnp.dot(hidden, w_second, preferred_element_type=jnp.float32).astype(jnp.bfloat16)
    coarse = convolve(second_proj, tile_cols, tile_counts, adjacency, myself).astype(jnp.bfloat16)
    answers = jnp.dot(
        got_hot.astype(jnp.bfloat16), coarse, preferred_element_type=jnp.float32
    ).astype(jnp.bfloat16)
    returned = lax.all_to_all(
        answers.reshape(device_count, DCAP, width), "nodes", split_axis=0, concat_axis=0, tiled=True
    ).reshape(remote_slots, width)
    value = (
        features.astype(jnp.float32)
        + jnp.dot(local_hot, coarse, preferred_element_type=jnp.float32)
        + jnp.dot(remote_hot, returned, preferred_element_type=jnp.float32)
    )
    return value.astype(jnp.bfloat16)


def solution(mesh):
    placed = (
        P("nodes", None),
        P("nodes"),
        P("nodes", None),
        P("nodes"),
        P("nodes", None, None, None),
        P(),
        P(),
    )
    return jax.shard_map(
        local, mesh=mesh, in_specs=placed, out_specs=P("nodes", None), check_vma=False
    )
```

```python
import jax
import jax.numpy as jnp
from jax import lax
from jax.sharding import PartitionSpec as P

DCAP = 4


def with_halo(block, sides, width):
    for axis, dim in sides:
        count = lax.axis_size(axis)
        forward = [(i, i + 1) for i in range(count - 1)]
        backward = [(target, source) for source, target in forward]
        low = lax.ppermute(
            lax.slice_in_dim(block, block.shape[dim] - width, None, axis=dim), axis, forward
        )
        high = lax.ppermute(lax.slice_in_dim(block, 0, width, axis=dim), axis, backward)
        block = jnp.concatenate([low, block, high], axis=dim)
    return block


def convolve(values, tile_cols, tile_counts, adjacency, myself):
    window = with_halo(values, (("nodes", 0),), values.shape[0])
    tile_size = adjacency.shape[2]
    per_device = tile_cols.shape[0]
    window_tiles = window.reshape(-1, tile_size, window.shape[1])
    offsets = tile_cols - (myself - 1) * per_device
    picked = window_tiles[offsets]
    live = jnp.arange(tile_cols.shape[1], dtype=jnp.int32)[None, :] < tile_counts[:, None]
    weights = jnp.where(live[:, :, None, None], adjacency, jnp.zeros((), adjacency.dtype))
    result = jnp.einsum("tkij,tkjf->tif", weights, picked, preferred_element_type=jnp.float32)
    return result.reshape(values.shape[0], values.shape[1])


def distinct_slots(owner_hot, lid_hot, clusters_here):
    contract_rows = (((0,), (0,)), ((), ()))
    presence = lax.dot_general(owner_hot, lid_hot, contract_rows, preferred_element_type=jnp.float32)
    named = (presence > 0).astype(jnp.bfloat16)
    lanes = jnp.arange(clusters_here, dtype=jnp.int32)
    before = (lanes[:, None] < lanes[None, :]).astype(jnp.bfloat16)
    rank = jnp.dot(named, before, preferred_element_type=jnp.float32)
    per_owner = jnp.dot(lid_hot, rank.T.astype(jnp.bfloat16), preferred_element_type=jnp.float32)
    slot = jnp.sum(per_owner * owner_hot.astype(jnp.float32), axis=1).astype(jnp.int32)
    return presence, rank, slot


def local(features, cluster_ids, tile_cols, tile_counts, adjacency, w_first, w_second):
    device_count = lax.axis_size("nodes")
    myself = lax.axis_index("nodes")
    fine_rows, width = features.shape
    clusters_here = adjacency.shape[0] * adjacency.shape[2]
    owners = cluster_ids // clusters_here
    lids = cluster_ids - owners * clusters_here
    remote = owners != myself
    peers = jnp.arange(device_count, dtype=jnp.int32)
    here = jnp.arange(clusters_here, dtype=jnp.int32)
    owner_hot = (owners[:, None] == peers[None, :]).astype(jnp.bfloat16)
    lid_hot = (lids[:, None] == here[None, :]).astype(jnp.bfloat16)
    presence, rank, slot = distinct_slots(owner_hot, lid_hot, clusters_here)
    remote_slots = device_count * DCAP
    slot_column = jnp.where(remote, owners * DCAP + slot, -1)
    slot_range = jnp.arange(remote_slots, dtype=jnp.int32)
    remote_hot = (slot_column[:, None] == slot_range[None, :]).astype(jnp.bfloat16)
    local_hot = jnp.where(remote[:, None], jnp.zeros((), jnp.bfloat16), lid_hot)
    contract_rows = (((0,), (0,)), ((), ()))
    remote_sums = lax.dot_general(
        remote_hot, features, contract_rows, preferred_element_type=jnp.float32
    )

    named = (presence > 0) & (peers != myself)[:, None]
    slot_counts = []
    slot_ids = []
    for k in range(DCAP):
        chosen = named & (rank == k)
        slot_counts.append(jnp.sum(jnp.where(chosen, presence, 0.0), axis=1))
        slot_ids.append(jnp.sum(jnp.where(chosen, here[None, :], 0), axis=1))
    slot_counts = jnp.stack(slot_counts, axis=1)
    slot_ids = jnp.stack(slot_ids, axis=1).astype(jnp.float32)
    meta = jnp.concatenate(
        [slot_counts, slot_ids, jnp.zeros((device_count, 128 - 2 * DCAP), jnp.float32)], axis=1
    )
    payload = jnp.concatenate([remote_sums.reshape(device_count, DCAP * width), meta], axis=1)
    got = lax.all_to_all(
        payload.reshape(device_count, 1, -1), "nodes", split_axis=0, concat_axis=0, tiled=True
    ).reshape(device_count, -1)
    got_sums = got[:, : DCAP * width].reshape(remote_slots, width)
    got_counts = got[:, DCAP * width : DCAP * width + DCAP].reshape(remote_slots)
    got_ids = got[:, DCAP * width + DCAP : DCAP * width + 2 * DCAP].reshape(remote_slots).astype(jnp.int32)
    local_sums = lax.dot_general(
        local_hot, features, contract_rows, preferred_element_type=jnp.float32
    )
    local_counts = lax.dynamic_index_in_dim(presence, myself, axis=0, keepdims=False)
    got_hot = (got_ids[:, None] == here[None, :]).astype(jnp.float32)
    sums_all = local_sums + lax.dot_general(
        got_hot, got_sums, contract_rows,
        precision=lax.Precision.HIGHEST, preferred_element_type=jnp.float32,
    )
    counts_all = local_counts + jnp.sum(got_hot * got_counts[:, None], axis=0)
    pooled = (sums_all / jnp.sqrt(counts_all + 1.0)[:, None]).astype(jnp.bfloat16)
    first_proj = jnp.dot(pooled, w_first, preferred_element_type=jnp.float32).astype(jnp.bfloat16)
    hidden = jnp.maximum(
        convolve(first_proj, tile_cols, tile_counts, adjacency, myself), 0.0
    ).astype(jnp.bfloat16)
    second_proj = jnp.dot(hidden, w_second, preferred_element_type=jnp.float32).astype(jnp.bfloat16)
    coarse = convolve(second_proj, tile_cols, tile_counts, adjacency, myself).astype(jnp.bfloat16)
    answers = jnp.dot(
        got_hot.astype(jnp.bfloat16), coarse, preferred_element_type=jnp.float32
    ).astype(jnp.bfloat16)
    returned = lax.all_to_all(
        answers.reshape(device_count, DCAP, width), "nodes", split_axis=0, concat_axis=0, tiled=True
    ).reshape(remote_slots, width)
    value = (
        features.astype(jnp.float32)
        + jnp.dot(local_hot, coarse, preferred_element_type=jnp.float32)
        + jnp.dot(remote_hot, returned, preferred_element_type=jnp.float32)
    )
    return value.astype(jnp.bfloat16)


def solution(mesh):
    placed = (
        P("nodes", None),
        P("nodes"),
        P("nodes", None),
        P("nodes"),
        P("nodes", None, None, None),
        P(),
        P(),
    )
    return jax.shard_map(
        local, mesh=mesh, in_specs=placed, out_specs=P("nodes", None), check_vma=False
    )
```

```python
import jax
import jax.numpy as jnp
from jax import lax
from jax.sharding import PartitionSpec as P

DCAP = 4


def with_halo(block, sides, width):
    for axis, dim in sides:
        count = lax.axis_size(axis)
        forward = [(i, i + 1) for i in range(count - 1)]
        backward = [(target, source) for source, target in forward]
        low = lax.ppermute(
            lax.slice_in_dim(block, block.shape[dim] - width, None, axis=dim), axis, forward
        )
        high = lax.ppermute(lax.slice_in_dim(block, 0, width, axis=dim), axis, backward)
        block = jnp.concatenate([low, block, high], axis=dim)
    return block


def convolve(values, tile_cols, tile_counts, adjacency, myself):
    window = with_halo(values, (("nodes", 0),), values.shape[0])
    tile_size = adjacency.shape[2]
    per_device = tile_cols.shape[0]
    window_tiles = window.reshape(-1, tile_size, window.shape[1])
    offsets = tile_cols - (myself - 1) * per_device
    picked = window_tiles[offsets]
    live = jnp.arange(tile_cols.shape[1], dtype=jnp.int32)[None, :] < tile_counts[:, None]
    weights = jnp.where(live[:, :, None, None], adjacency, jnp.zeros((), adjacency.dtype))
    result = jnp.einsum("tkij,tkjf->tif", weights, picked, preferred_element_type=jnp.float32)
    return result.reshape(values.shape[0], values.shape[1])


def distinct_slots(owner_hot, lid_hot, clusters_here):
    contract_rows = (((0,), (0,)), ((), ()))
    presence = lax.dot_general(owner_hot, lid_hot, contract_rows, preferred_element_type=jnp.float32)
    named = (presence > 0).astype(jnp.bfloat16)
    lanes = jnp.arange(clusters_here, dtype=jnp.int32)
    before = (lanes[:, None] < lanes[None, :]).astype(jnp.bfloat16)
    rank = jnp.dot(named, before, preferred_element_type=jnp.float32)
    return presence, rank


def local(features, cluster_ids, tile_cols, tile_counts, adjacency, w_first, w_second):
    device_count = lax.axis_size("nodes")
    myself = lax.axis_index("nodes")
    fine_rows, width = features.shape
    clusters_here = adjacency.shape[0] * adjacency.shape[2]
    owners = cluster_ids // clusters_here
    lids = cluster_ids - owners * clusters_here
    remote = owners != myself
    peers = jnp.arange(device_count, dtype=jnp.int32)
    here = jnp.arange(clusters_here, dtype=jnp.int32)
    owner_hot = (owners[:, None] == peers[None, :]).astype(jnp.bfloat16)
    lid_hot = (lids[:, None] == here[None, :]).astype(jnp.bfloat16)
    presence, rank = distinct_slots(owner_hot, lid_hot, clusters_here)
    remote_slots = device_count * DCAP
    contract_rows = (((0,), (0,)), ((), ()))

    named = (presence > 0) & (peers != myself)[:, None]
    slot_counts = []
    slot_ids = []
    for k in range(DCAP):
        chosen = named & (rank == k)
        slot_counts.append(jnp.sum(jnp.where(chosen, presence, 0.0), axis=1))
        found = jnp.sum(jnp.where(chosen, here[None, :], 0), axis=1)
        slot_ids.append(jnp.where(jnp.any(chosen, axis=1), found, clusters_here))
    slot_counts = jnp.stack(slot_counts, axis=1)
    slot_ids = jnp.stack(slot_ids, axis=1)
    split = jnp.concatenate([slot_ids // 32, slot_ids % 32], axis=1).astype(jnp.bfloat16)
    parts = jnp.dot(owner_hot, split, preferred_element_type=jnp.float32).astype(jnp.int32)
    lows = parts[:, :DCAP] * 32 + parts[:, DCAP:]
    slot = jnp.sum((lids[:, None] >= lows[:, 1:]).astype(jnp.int32), axis=1)
    slot = jnp.where(remote, slot, -1)
    masked = jnp.concatenate(
        [jnp.where((slot == k)[:, None], features, jnp.zeros((), features.dtype)) for k in range(DCAP)],
        axis=1,
    )
    remote_sums = lax.dot_general(owner_hot, masked, contract_rows, preferred_element_type=jnp.float32)
    meta = jnp.concatenate(
        [slot_counts, jnp.where(slot_ids < clusters_here, slot_ids, 0).astype(jnp.float32),
         jnp.zeros((device_count, 128 - 2 * DCAP), jnp.float32)],
        axis=1,
    )
    payload = jnp.concatenate([remote_sums, meta], axis=1)
    got = lax.all_to_all(
        payload.reshape(device_count, 1, -1), "nodes", split_axis=0, concat_axis=0, tiled=True
    ).reshape(device_count, -1)
    got_sums = got[:, : DCAP * width].reshape(remote_slots, width)
    got_counts = got[:, DCAP * width : DCAP * width + DCAP].reshape(remote_slots)
    got_ids = got[:, DCAP * width + DCAP : DCAP * width + 2 * DCAP].reshape(remote_slots).astype(jnp.int32)
    local_hot = jnp.where(remote[:, None], jnp.zeros((), jnp.bfloat16), lid_hot)
    slot_column = jnp.where(remote, owners * DCAP + slot, -1)
    slot_range = jnp.arange(remote_slots, dtype=jnp.int32)
    remote_hot = (slot_column[:, None] == slot_range[None, :]).astype(jnp.bfloat16)
    local_sums = lax.dot_general(
        local_hot, features, contract_rows, preferred_element_type=jnp.float32
    )
    local_counts = lax.dynamic_index_in_dim(presence, myself, axis=0, keepdims=False)
    got_hot = (got_ids[:, None] == here[None, :]).astype(jnp.float32)
    sums_all = local_sums + lax.dot_general(
        got_hot, got_sums, contract_rows,
        precision=lax.Precision.HIGHEST, preferred_element_type=jnp.float32,
    )
    counts_all = local_counts + jnp.sum(got_hot * got_counts[:, None], axis=0)
    pooled = (sums_all / jnp.sqrt(counts_all + 1.0)[:, None]).astype(jnp.bfloat16)
    first_proj = jnp.dot(pooled, w_first, preferred_element_type=jnp.float32).astype(jnp.bfloat16)
    hidden = jnp.maximum(
        convolve(first_proj, tile_cols, tile_counts, adjacency, myself), 0.0
    ).astype(jnp.bfloat16)
    second_proj = jnp.dot(hidden, w_second, preferred_element_type=jnp.float32).astype(jnp.bfloat16)
    coarse = convolve(second_proj, tile_cols, tile_counts, adjacency, myself).astype(jnp.bfloat16)
    answers = jnp.dot(
        got_hot.astype(jnp.bfloat16), coarse, preferred_element_type=jnp.float32
    ).astype(jnp.bfloat16)
    returned = lax.all_to_all(
        answers.reshape(device_count, DCAP, width), "nodes", split_axis=0, concat_axis=0, tiled=True
    ).reshape(remote_slots, width)
    first = (
        features.astype(jnp.float32) + jnp.dot(local_hot, coarse, preferred_element_type=jnp.float32)
    ).astype(jnp.bfloat16)
    value = first.astype(jnp.float32) + jnp.dot(remote_hot, returned, preferred_element_type=jnp.float32)
    return value.astype(jnp.bfloat16)


def solution(mesh):
    placed = (
        P("nodes", None),
        P("nodes"),
        P("nodes", None),
        P("nodes"),
        P("nodes", None, None, None),
        P(),
        P(),
    )
    return jax.shard_map(
        local, mesh=mesh, in_specs=placed, out_specs=P("nodes", None), check_vma=False
    )
```

```python
import jax
import jax.numpy as jnp
from jax import lax
from jax.sharding import PartitionSpec as P

DCAP = 4


def with_halo(block, sides, width):
    for axis, dim in sides:
        count = lax.axis_size(axis)
        forward = [(i, i + 1) for i in range(count - 1)]
        backward = [(target, source) for source, target in forward]
        low = lax.ppermute(
            lax.slice_in_dim(block, block.shape[dim] - width, None, axis=dim), axis, forward
        )
        high = lax.ppermute(lax.slice_in_dim(block, 0, width, axis=dim), axis, backward)
        block = jnp.concatenate([low, block, high], axis=dim)
    return block


def convolve(values, tile_cols, tile_counts, adjacency, myself):
    window = with_halo(values, (("nodes", 0),), values.shape[0])
    tile_size = adjacency.shape[2]
    per_device = tile_cols.shape[0]
    window_tiles = window.reshape(-1, tile_size, window.shape[1])
    offsets = tile_cols - (myself - 1) * per_device
    picked = window_tiles[offsets]
    live = jnp.arange(tile_cols.shape[1], dtype=jnp.int32)[None, :] < tile_counts[:, None]
    weights = jnp.where(live[:, :, None, None], adjacency, jnp.zeros((), adjacency.dtype))
    result = jnp.einsum("tkij,tkjf->tif", weights, picked, preferred_element_type=jnp.float32)
    return result.reshape(values.shape[0], values.shape[1])


def distinct_slots(owner_hot, lid_hot, clusters_here):
    contract_rows = (((0,), (0,)), ((), ()))
    presence = lax.dot_general(owner_hot, lid_hot, contract_rows, preferred_element_type=jnp.float32)
    named = (presence > 0).astype(jnp.bfloat16)
    lanes = jnp.arange(clusters_here, dtype=jnp.int32)
    before = (lanes[:, None] < lanes[None, :]).astype(jnp.bfloat16)
    rank = jnp.dot(named, before, preferred_element_type=jnp.float32)
    return presence, rank


def local(features, cluster_ids, tile_cols, tile_counts, adjacency, w_first, w_second):
    device_count = lax.axis_size("nodes")
    myself = lax.axis_index("nodes")
    fine_rows, width = features.shape
    clusters_here = adjacency.shape[0] * adjacency.shape[2]
    owners = cluster_ids // clusters_here
    lids = cluster_ids - owners * clusters_here
    remote = owners != myself
    peers = jnp.arange(device_count, dtype=jnp.int32)
    here = jnp.arange(clusters_here, dtype=jnp.int32)
    owner_hot = (owners[:, None] == peers[None, :]).astype(jnp.bfloat16)
    lid_hot = (lids[:, None] == here[None, :]).astype(jnp.bfloat16)
    presence, rank = distinct_slots(owner_hot, lid_hot, clusters_here)
    remote_slots = device_count * DCAP
    contract_rows = (((0,), (0,)), ((), ()))

    named = (presence > 0) & (peers != myself)[:, None]
    slot_counts = []
    slot_ids = []
    for k in range(DCAP):
        chosen = named & (rank == k)
        slot_counts.append(jnp.sum(jnp.where(chosen, presence, 0.0), axis=1))
        found = jnp.sum(jnp.where(chosen, here[None, :], 0), axis=1)
        slot_ids.append(jnp.where(jnp.any(chosen, axis=1), found, clusters_here))
    slot_counts = jnp.stack(slot_counts, axis=1)
    slot_ids = jnp.stack(slot_ids, axis=1)
    split = jnp.concatenate([slot_ids // 32, slot_ids % 32], axis=1).astype(jnp.bfloat16)
    parts = jnp.dot(owner_hot, split, preferred_element_type=jnp.float32).astype(jnp.int32)
    lows = parts[:, :DCAP] * 32 + parts[:, DCAP:]
    slot = jnp.sum((lids[:, None] >= lows[:, 1:]).astype(jnp.int32), axis=1)
    slot = jnp.where(remote, slot, -1)
    slot_hot = [jnp.where((slot == k)[:, None], owner_hot, jnp.zeros((), owner_hot.dtype)) for k in range(DCAP)]
    remote_sums = jnp.concatenate(
        [lax.dot_general(hot, features, contract_rows, preferred_element_type=jnp.float32) for hot in slot_hot],
        axis=1,
    )
    meta = jnp.concatenate(
        [slot_counts, jnp.where(slot_ids < clusters_here, slot_ids, 0).astype(jnp.float32),
         jnp.zeros((device_count, 128 - 2 * DCAP), jnp.float32)],
        axis=1,
    )
    payload = jnp.concatenate([remote_sums, meta], axis=1)
    got = lax.all_to_all(
        payload.reshape(device_count, 1, -1), "nodes", split_axis=0, concat_axis=0, tiled=True
    ).reshape(device_count, -1)
    got_sums = got[:, : DCAP * width].reshape(remote_slots, width)
    got_counts = got[:, DCAP * width : DCAP * width + DCAP].reshape(remote_slots)
    got_ids = got[:, DCAP * width + DCAP : DCAP * width + 2 * DCAP].reshape(remote_slots).astype(jnp.int32)
    local_hot = jnp.where(remote[:, None], jnp.zeros((), jnp.bfloat16), lid_hot)
    local_sums = lax.dot_general(
        local_hot, features, contract_rows, preferred_element_type=jnp.float32
    )
    local_counts = lax.dynamic_index_in_dim(presence, myself, axis=0, keepdims=False)
    got_hot = (got_ids[:, None] == here[None, :]).astype(jnp.float32)
    sums_all = local_sums + lax.dot_general(
        got_hot, got_sums, contract_rows,
        precision=lax.Precision.HIGHEST, preferred_element_type=jnp.float32,
    )
    counts_all = local_counts + jnp.sum(got_hot * got_counts[:, None], axis=0)
    pooled = (sums_all / jnp.sqrt(counts_all + 1.0)[:, None]).astype(jnp.bfloat16)
    first_proj = jnp.dot(pooled, w_first, preferred_element_type=jnp.float32).astype(jnp.bfloat16)
    hidden = jnp.maximum(
        convolve(first_proj, tile_cols, tile_counts, adjacency, myself), 0.0
    ).astype(jnp.bfloat16)
    second_proj = jnp.dot(hidden, w_second, preferred_element_type=jnp.float32).astype(jnp.bfloat16)
    coarse = convolve(second_proj, tile_cols, tile_counts, adjacency, myself).astype(jnp.bfloat16)
    answers = jnp.dot(
        got_hot.astype(jnp.bfloat16), coarse, preferred_element_type=jnp.float32
    ).astype(jnp.bfloat16)
    returned = lax.all_to_all(
        answers.reshape(device_count, DCAP, width), "nodes", split_axis=0, concat_axis=0, tiled=True
    )
    first = (
        features.astype(jnp.float32) + jnp.dot(local_hot, coarse, preferred_element_type=jnp.float32)
    ).astype(jnp.bfloat16)
    value = first.astype(jnp.float32)
    for k in range(DCAP):
        value = value + jnp.dot(slot_hot[k], returned[:, k, :], preferred_element_type=jnp.float32)
    return value.astype(jnp.bfloat16)


def solution(mesh):
    placed = (
        P("nodes", None),
        P("nodes"),
        P("nodes", None),
        P("nodes"),
        P("nodes", None, None, None),
        P(),
        P(),
    )
    return jax.shard_map(
        local, mesh=mesh, in_specs=placed, out_specs=P("nodes", None), check_vma=False
    )
```

```python
import jax
import jax.numpy as jnp
from jax import lax
from jax.sharding import PartitionSpec as P

DCAP = 4


def with_halo(block, sides, width):
    for axis, dim in sides:
        count = lax.axis_size(axis)
        forward = [(i, i + 1) for i in range(count - 1)]
        backward = [(target, source) for source, target in forward]
        low = lax.ppermute(
            lax.slice_in_dim(block, block.shape[dim] - width, None, axis=dim), axis, forward
        )
        high = lax.ppermute(lax.slice_in_dim(block, 0, width, axis=dim), axis, backward)
        block = jnp.concatenate([low, block, high], axis=dim)
    return block


def convolve(values, tile_cols, tile_counts, adjacency, myself):
    window = with_halo(values, (("nodes", 0),), values.shape[0])
    tile_size = adjacency.shape[2]
    per_device = tile_cols.shape[0]
    window_tiles = window.reshape(-1, tile_size, window.shape[1])
    offsets = tile_cols - (myself - 1) * per_device
    picked = window_tiles[offsets]
    live = jnp.arange(tile_cols.shape[1], dtype=jnp.int32)[None, :] < tile_counts[:, None]
    weights = jnp.where(live[:, :, None, None], adjacency, jnp.zeros((), adjacency.dtype))
    result = jnp.einsum("tkij,tkjf->tif", weights, picked, preferred_element_type=jnp.float32)
    return result.reshape(values.shape[0], values.shape[1])


def distinct_slots(owner_hot, lid_hot, clusters_here):
    contract_rows = (((0,), (0,)), ((), ()))
    presence = lax.dot_general(owner_hot, lid_hot, contract_rows, preferred_element_type=jnp.float32)
    named = (presence > 0).astype(jnp.bfloat16)
    lanes = jnp.arange(clusters_here, dtype=jnp.int32)
    before = (lanes[:, None] < lanes[None, :]).astype(jnp.bfloat16)
    rank = jnp.dot(named, before, preferred_element_type=jnp.float32)
    return presence, rank


def local(features, cluster_ids, tile_cols, tile_counts, adjacency, w_first, w_second):
    device_count = lax.axis_size("nodes")
    myself = lax.axis_index("nodes")
    fine_rows, width = features.shape
    clusters_here = adjacency.shape[0] * adjacency.shape[2]
    owners = cluster_ids // clusters_here
    lids = cluster_ids - owners * clusters_here
    remote = owners != myself
    peers = jnp.arange(device_count, dtype=jnp.int32)
    here = jnp.arange(clusters_here, dtype=jnp.int32)
    owner_hot = (owners[:, None] == peers[None, :]).astype(jnp.bfloat16)
    lid_hot = (lids[:, None] == here[None, :]).astype(jnp.bfloat16)
    presence, rank = distinct_slots(owner_hot, lid_hot, clusters_here)
    remote_slots = device_count * DCAP
    contract_rows = (((0,), (0,)), ((), ()))

    named = (presence > 0) & (peers != myself)[:, None]
    slot_counts = []
    slot_ids = []
    for k in range(DCAP):
        chosen = named & (rank == k)
        slot_counts.append(jnp.sum(jnp.where(chosen, presence, 0.0), axis=1))
        found = jnp.sum(jnp.where(chosen, here[None, :], 0), axis=1)
        slot_ids.append(jnp.where(jnp.any(chosen, axis=1), found, clusters_here))
    slot_counts = jnp.stack(slot_counts, axis=1)
    slot_ids = jnp.stack(slot_ids, axis=1)
    split = jnp.concatenate([slot_ids // 32, slot_ids % 32], axis=1).astype(jnp.bfloat16)
    parts = jnp.dot(owner_hot, split, preferred_element_type=jnp.float32).astype(jnp.int32)
    lows = parts[:, :DCAP] * 32 + parts[:, DCAP:]
    slot = jnp.sum((lids[:, None] >= lows[:, 1:]).astype(jnp.int32), axis=1)
    slot = jnp.where(remote, slot, -1)
    slot_column = jnp.where(remote, owners * DCAP + slot, -1)
    slot_range = jnp.arange(remote_slots, dtype=jnp.int32)
    remote_hot = (slot_column[:, None] == slot_range[None, :]).astype(jnp.bfloat16)
    remote_sums = lax.dot_general(remote_hot, features, contract_rows, preferred_element_type=jnp.float32)
    got_sums = lax.all_to_all(
        remote_sums.reshape(device_count, DCAP, width), "nodes", split_axis=0, concat_axis=0, tiled=True
    ).reshape(remote_slots, width)
    meta = jnp.concatenate([slot_counts, slot_ids.astype(jnp.float32)], axis=1)
    every_meta = lax.all_gather(meta[None], "nodes", axis=0, tiled=True)
    mine = lax.dynamic_index_in_dim(every_meta, myself, axis=1, keepdims=False)
    got_counts = mine[:, :DCAP].reshape(remote_slots)
    got_ids = jnp.where(mine[:, DCAP:] < clusters_here, mine[:, DCAP:], 0).reshape(remote_slots).astype(jnp.int32)
    local_hot = jnp.where(remote[:, None], jnp.zeros((), jnp.bfloat16), lid_hot)
    local_sums = lax.dot_general(
        local_hot, features, contract_rows, preferred_element_type=jnp.float32
    )
    local_counts = lax.dynamic_index_in_dim(presence, myself, axis=0, keepdims=False)
    got_hot = (got_ids[:, None] == here[None, :]).astype(jnp.float32)
    sums_all = local_sums + lax.dot_general(
        got_hot, got_sums, contract_rows,
        precision=lax.Precision.HIGHEST, preferred_element_type=jnp.float32,
    )
    counts_all = local_counts + jnp.sum(got_hot * got_counts[:, None], axis=0)
    pooled = (sums_all / jnp.sqrt(counts_all + 1.0)[:, None]).astype(jnp.bfloat16)
    first_proj = jnp.dot(pooled, w_first, preferred_element_type=jnp.float32).astype(jnp.bfloat16)
    hidden = jnp.maximum(
        convolve(first_proj, tile_cols, tile_counts, adjacency, myself), 0.0
    ).astype(jnp.bfloat16)
    second_proj = jnp.dot(hidden, w_second, preferred_element_type=jnp.float32).astype(jnp.bfloat16)
    coarse = convolve(second_proj, tile_cols, tile_counts, adjacency, myself).astype(jnp.bfloat16)
    answers = jnp.dot(
        got_hot.astype(jnp.bfloat16), coarse, preferred_element_type=jnp.float32
    ).astype(jnp.bfloat16)
    returned = lax.all_to_all(
        answers.reshape(device_count, DCAP, width), "nodes", split_axis=0, concat_axis=0, tiled=True
    )
    first = (
        features.astype(jnp.float32) + jnp.dot(local_hot, coarse, preferred_element_type=jnp.float32)
    ).astype(jnp.bfloat16)
    value = first.astype(jnp.float32) + jnp.dot(
        remote_hot, returned.reshape(remote_slots, width), preferred_element_type=jnp.float32
    )
    return value.astype(jnp.bfloat16)


def solution(mesh):
    placed = (
        P("nodes", None),
        P("nodes"),
        P("nodes", None),
        P("nodes"),
        P("nodes", None, None, None),
        P(),
        P(),
    )
    return jax.shard_map(
        local, mesh=mesh, in_specs=placed, out_specs=P("nodes", None), check_vma=False
    )
```

```python
import jax
import jax.numpy as jnp
from jax import lax
from jax.sharding import PartitionSpec as P

DCAP = 4


def with_halo(block, sides, width):
    for axis, dim in sides:
        count = lax.axis_size(axis)
        forward = [(i, i + 1) for i in range(count - 1)]
        backward = [(target, source) for source, target in forward]
        low = lax.ppermute(
            lax.slice_in_dim(block, block.shape[dim] - width, None, axis=dim), axis, forward
        )
        high = lax.ppermute(lax.slice_in_dim(block, 0, width, axis=dim), axis, backward)
        block = jnp.concatenate([low, block, high], axis=dim)
    return block


def convolve(values, tile_cols, tile_counts, adjacency, myself):
    window = with_halo(values, (("nodes", 0),), values.shape[0])
    tile_size = adjacency.shape[2]
    per_device = tile_cols.shape[0]
    window_tiles = window.reshape(-1, tile_size, window.shape[1])
    offsets = tile_cols - (myself - 1) * per_device
    picked = window_tiles[offsets]
    live = jnp.arange(tile_cols.shape[1], dtype=jnp.int32)[None, :] < tile_counts[:, None]
    weights = jnp.where(live[:, :, None, None], adjacency, jnp.zeros((), adjacency.dtype))
    result = jnp.einsum("tkij,tkjf->tif", weights, picked, preferred_element_type=jnp.float32)
    return result.reshape(values.shape[0], values.shape[1])


def distinct_slots(owner_hot, lid_hot, clusters_here):
    contract_rows = (((0,), (0,)), ((), ()))
    presence = lax.dot_general(owner_hot, lid_hot, contract_rows, preferred_element_type=jnp.float32)
    named = (presence > 0).astype(jnp.bfloat16)
    lanes = jnp.arange(clusters_here, dtype=jnp.int32)
    before = (lanes[:, None] < lanes[None, :]).astype(jnp.bfloat16)
    rank = jnp.dot(named, before, preferred_element_type=jnp.float32)
    return presence, rank


def local(features, cluster_ids, tile_cols, tile_counts, adjacency, w_first, w_second):
    device_count = lax.axis_size("nodes")
    myself = lax.axis_index("nodes")
    fine_rows, width = features.shape
    clusters_here = adjacency.shape[0] * adjacency.shape[2]
    owners = cluster_ids // clusters_here
    lids = cluster_ids - owners * clusters_here
    remote = owners != myself
    peers = jnp.arange(device_count, dtype=jnp.int32)
    here = jnp.arange(clusters_here, dtype=jnp.int32)
    owner_hot = (owners[:, None] == peers[None, :]).astype(jnp.bfloat16)
    lid_hot = (lids[:, None] == here[None, :]).astype(jnp.bfloat16)
    presence, rank = distinct_slots(owner_hot, lid_hot, clusters_here)

    named = (presence > 0) & (peers != myself)[:, None]
    slot_counts = []
    slot_ids = []
    for k in range(DCAP):
        chosen = named & (rank == k)
        slot_counts.append(jnp.sum(jnp.where(chosen, presence, 0.0), axis=1))
        found = jnp.sum(jnp.where(chosen, here[None, :], 0), axis=1)
        slot_ids.append(jnp.where(jnp.any(chosen, axis=1), found, clusters_here))
    slot_counts = jnp.stack(slot_counts, axis=1)
    slot_ids = jnp.stack(slot_ids, axis=1)
    split = jnp.concatenate([slot_ids // 32, slot_ids % 32], axis=1).astype(jnp.bfloat16)
    parts = jnp.dot(owner_hot, split, preferred_element_type=jnp.float32).astype(jnp.int32)
    lows = parts[:, :DCAP] * 32 + parts[:, DCAP:]
    slot = jnp.sum((lids[:, None] >= lows[:, 1:]).astype(jnp.int32), axis=1)
    remote_slots = device_count * DCAP
    slot_column = jnp.where(remote, owners * DCAP + slot, -1)
    slot_range = jnp.arange(remote_slots, dtype=jnp.int32)
    remote_hot = (slot_column[:, None] == slot_range[None, :]).astype(jnp.bfloat16)
    local_hot = jnp.where(remote[:, None], jnp.zeros((), jnp.bfloat16), lid_hot)
    contract_rows = (((0,), (0,)), ((), ()))
    remote_sums = lax.dot_general(
        remote_hot, features, contract_rows, preferred_element_type=jnp.float32
    )

    meta = jnp.concatenate(
        [slot_counts, jnp.where(slot_ids < clusters_here, slot_ids, 0).astype(jnp.float32),
         jnp.zeros((device_count, 128 - 2 * DCAP), jnp.float32)],
        axis=1,
    )
    payload = jnp.concatenate([remote_sums.reshape(device_count, DCAP * width), meta], axis=1)
    got = lax.all_to_all(
        payload.reshape(device_count, 1, -1), "nodes", split_axis=0, concat_axis=0, tiled=True
    ).reshape(device_count, -1)
    got_sums = got[:, : DCAP * width].reshape(remote_slots, width)
    got_counts = got[:, DCAP * width : DCAP * width + DCAP].reshape(remote_slots)
    got_ids = got[:, DCAP * width + DCAP : DCAP * width + 2 * DCAP].reshape(remote_slots).astype(jnp.int32)
    local_sums = lax.dot_general(
        local_hot, features, contract_rows, preferred_element_type=jnp.float32
    )
    local_counts = lax.dynamic_index_in_dim(presence, myself, axis=0, keepdims=False)
    got_hot = (got_ids[:, None] == here[None, :]).astype(jnp.float32)
    sums_all = local_sums + lax.dot_general(
        got_hot, got_sums, contract_rows,
        precision=lax.Precision.HIGHEST, preferred_element_type=jnp.float32,
    )
    counts_all = local_counts + jnp.sum(got_hot * got_counts[:, None], axis=0)
    pooled = (sums_all / jnp.sqrt(counts_all + 1.0)[:, None]).astype(jnp.bfloat16)
    first_proj = jnp.dot(pooled, w_first, preferred_element_type=jnp.float32).astype(jnp.bfloat16)
    hidden = jnp.maximum(
        convolve(first_proj, tile_cols, tile_counts, adjacency, myself), 0.0
    ).astype(jnp.bfloat16)
    second_proj = jnp.dot(hidden, w_second, preferred_element_type=jnp.float32).astype(jnp.bfloat16)
    coarse = convolve(second_proj, tile_cols, tile_counts, adjacency, myself).astype(jnp.bfloat16)
    answers = jnp.dot(
        got_hot.astype(jnp.bfloat16), coarse, preferred_element_type=jnp.float32
    ).astype(jnp.bfloat16)
    returned = lax.all_to_all(
        answers.reshape(device_count, DCAP, width), "nodes", split_axis=0, concat_axis=0, tiled=True
    ).reshape(remote_slots, width)
    value = (
        features.astype(jnp.float32)
        + jnp.dot(local_hot, coarse, preferred_element_type=jnp.float32)
        + jnp.dot(remote_hot, returned, preferred_element_type=jnp.float32)
    )
    return value.astype(jnp.bfloat16)


def solution(mesh):
    placed = (
        P("nodes", None),
        P("nodes"),
        P("nodes", None),
        P("nodes"),
        P("nodes", None, None, None),
        P(),
        P(),
    )
    return jax.shard_map(
        local, mesh=mesh, in_specs=placed, out_specs=P("nodes", None), check_vma=False
    )
```

```python
import jax
import jax.numpy as jnp
from jax import lax
from jax.sharding import PartitionSpec as P

DCAP = 4


def with_halo(block, sides, width):
    for axis, dim in sides:
        count = lax.axis_size(axis)
        forward = [(i, i + 1) for i in range(count - 1)]
        backward = [(target, source) for source, target in forward]
        low = lax.ppermute(
            lax.slice_in_dim(block, block.shape[dim] - width, None, axis=dim), axis, forward
        )
        high = lax.ppermute(lax.slice_in_dim(block, 0, width, axis=dim), axis, backward)
        block = jnp.concatenate([low, block, high], axis=dim)
    return block


def convolve(values, tile_cols, tile_counts, adjacency, myself):
    window = with_halo(values, (("nodes", 0),), values.shape[0])
    tile_size = adjacency.shape[2]
    per_device = tile_cols.shape[0]
    window_tiles = window.reshape(-1, tile_size, window.shape[1])
    offsets = tile_cols - (myself - 1) * per_device
    picked = window_tiles[offsets]
    live = jnp.arange(tile_cols.shape[1], dtype=jnp.int32)[None, :] < tile_counts[:, None]
    weights = jnp.where(live[:, :, None, None], adjacency, jnp.zeros((), adjacency.dtype))
    result = jnp.einsum("tkij,tkjf->tif", weights, picked, preferred_element_type=jnp.float32)
    return result.reshape(values.shape[0], values.shape[1])


def distinct_slots(owner_hot, lid_hot, clusters_here):
    contract_rows = (((0,), (0,)), ((), ()))
    presence = lax.dot_general(owner_hot, lid_hot, contract_rows, preferred_element_type=jnp.float32)
    named = (presence > 0).astype(jnp.bfloat16)
    lanes = jnp.arange(clusters_here, dtype=jnp.int32)
    before = (lanes[:, None] < lanes[None, :]).astype(jnp.bfloat16)
    rank = jnp.dot(named, before, preferred_element_type=jnp.float32)
    return presence, rank


def local(features, cluster_ids, tile_cols, tile_counts, adjacency, w_first, w_second):
    device_count = lax.axis_size("nodes")
    myself = lax.axis_index("nodes")
    fine_rows, width = features.shape
    clusters_here = adjacency.shape[0] * adjacency.shape[2]
    owners = cluster_ids // clusters_here
    lids = cluster_ids - owners * clusters_here
    remote = owners != myself
    peers = jnp.arange(device_count, dtype=jnp.int32)
    here = jnp.arange(clusters_here, dtype=jnp.int32)
    owner_hot = (owners[:, None] == peers[None, :]).astype(jnp.bfloat16)
    lid_hot = (lids[:, None] == here[None, :]).astype(jnp.bfloat16)
    presence, rank = distinct_slots(owner_hot, lid_hot, clusters_here)

    named = (presence > 0) & (peers != myself)[:, None]
    slot_counts = []
    slot_ids = []
    for k in range(DCAP):
        chosen = named & (rank == k)
        slot_counts.append(jnp.sum(jnp.where(chosen, presence, 0.0), axis=1))
        found = jnp.sum(jnp.where(chosen, here[None, :], 0), axis=1)
        slot_ids.append(jnp.where(jnp.any(chosen, axis=1), found, clusters_here))
    slot_counts = jnp.stack(slot_counts, axis=1)
    slot_ids = jnp.stack(slot_ids, axis=1)
    split = jnp.concatenate([slot_ids // 32, slot_ids % 32], axis=1).astype(jnp.bfloat16)
    parts = jnp.dot(owner_hot, split, preferred_element_type=jnp.float32).astype(jnp.int32)
    lows = parts[:, :DCAP] * 32 + parts[:, DCAP:]
    slot = jnp.sum((lids[:, None] >= lows[:, 1:]).astype(jnp.int32), axis=1)
    remote_slots = device_count * DCAP
    slot_column = jnp.where(remote, owners * DCAP + slot, -1)
    slot_range = jnp.arange(remote_slots, dtype=jnp.int32)
    remote_hot = (slot_column[:, None] == slot_range[None, :]).astype(jnp.bfloat16)
    local_hot = jnp.where(remote[:, None], jnp.zeros((), jnp.bfloat16), lid_hot)
    contract_rows = (((0,), (0,)), ((), ()))
    remote_sums = lax.dot_general(
        remote_hot, features, contract_rows, preferred_element_type=jnp.float32
    )

    meta = jnp.concatenate(
        [slot_counts, jnp.where(slot_ids < clusters_here, slot_ids, 0).astype(jnp.float32),
         jnp.zeros((device_count, 128 - 2 * DCAP), jnp.float32)],
        axis=1,
    )
    payload = jnp.concatenate([remote_sums.reshape(device_count, DCAP * width), meta], axis=1)
    got = lax.all_to_all(
        payload.reshape(device_count, 1, -1), "nodes", split_axis=0, concat_axis=0, tiled=True
    ).reshape(device_count, -1)
    got_sums = got[:, : DCAP * width].reshape(remote_slots, width)
    got_counts = got[:, DCAP * width : DCAP * width + DCAP].reshape(remote_slots)
    got_ids = got[:, DCAP * width + DCAP : DCAP * width + 2 * DCAP].reshape(remote_slots).astype(jnp.int32)
    local_sums = lax.dot_general(
        local_hot, features, contract_rows, preferred_element_type=jnp.float32
    )
    local_counts = lax.dynamic_index_in_dim(presence, myself, axis=0, keepdims=False)
    got_hot = (got_ids[:, None] == here[None, :]).astype(jnp.float32)
    sums_all = local_sums + lax.dot_general(
        got_hot, got_sums, contract_rows,
        precision=lax.Precision.HIGHEST, preferred_element_type=jnp.float32,
    )
    counts_all = local_counts + jnp.sum(got_hot * got_counts[:, None], axis=0)
    pooled = (sums_all / jnp.sqrt(counts_all + 1.0)[:, None]).astype(jnp.bfloat16)
    first_proj = jnp.dot(pooled, w_first, preferred_element_type=jnp.float32).astype(jnp.bfloat16)
    hidden = jnp.maximum(
        convolve(first_proj, tile_cols, tile_counts, adjacency, myself), 0.0
    ).astype(jnp.bfloat16)
    second_proj = jnp.dot(hidden, w_second, preferred_element_type=jnp.float32).astype(jnp.bfloat16)
    coarse = convolve(second_proj, tile_cols, tile_counts, adjacency, myself).astype(jnp.bfloat16)
    answers = jnp.dot(
        got_hot.astype(jnp.bfloat16), coarse, preferred_element_type=jnp.float32
    ).astype(jnp.bfloat16)
    returned = lax.all_to_all(
        answers.reshape(device_count, DCAP, width), "nodes", split_axis=0, concat_axis=0, tiled=True
    ).reshape(remote_slots, width)
    table = jnp.concatenate([coarse, returned], axis=0)
    column = jnp.where(remote, clusters_here + slot_column, lids)
    columns = jnp.arange(clusters_here + remote_slots, dtype=jnp.int32)
    one_hot = (column[:, None] == columns[None, :]).astype(jnp.bfloat16)
    value = features.astype(jnp.float32) + jnp.dot(one_hot, table, preferred_element_type=jnp.float32)
    return value.astype(jnp.bfloat16)


def solution(mesh):
    placed = (
        P("nodes", None),
        P("nodes"),
        P("nodes", None),
        P("nodes"),
        P("nodes", None, None, None),
        P(),
        P(),
    )
    return jax.shard_map(
        local, mesh=mesh, in_specs=placed, out_specs=P("nodes", None), check_vma=False
    )
```

```python
import jax
import jax.numpy as jnp
from jax import lax
from jax.experimental import pallas as pl
from jax.sharding import PartitionSpec as P

DCAP = 4


def unpool_kernel(col_ref, x_ref, table_ref, out_ref):
    cols = lax.broadcasted_iota(jnp.int32, (col_ref.shape[0], table_ref.shape[0]), 1)
    one_hot = (col_ref[...] == cols).astype(table_ref.dtype)
    picked = jnp.dot(one_hot, table_ref[...], preferred_element_type=jnp.float32)
    out_ref[...] = (x_ref[...].astype(jnp.float32) + picked).astype(out_ref.dtype)


def add_rows(column, rows, table, block=512):
    count, width = rows.shape
    return pl.pallas_call(
        unpool_kernel,
        grid=(count // block,),
        in_specs=[
            pl.BlockSpec((block, 1), lambda i: (i, 0)),
            pl.BlockSpec((block, width), lambda i: (i, 0)),
            pl.BlockSpec(table.shape, lambda i: (0, 0)),
        ],
        out_specs=pl.BlockSpec((block, width), lambda i: (i, 0)),
        out_shape=jax.ShapeDtypeStruct(rows.shape, rows.dtype),
        cost_estimate=pl.CostEstimate(
            flops=2 * count * table.shape[0] * width,
            transcendentals=0,
            bytes_accessed=4 * count * width + 4 * count + 2 * table.size,
        ),
    )(column.reshape(count, 1), rows, table)


def with_halo(block, sides, width):
    for axis, dim in sides:
        count = lax.axis_size(axis)
        forward = [(i, i + 1) for i in range(count - 1)]
        backward = [(target, source) for source, target in forward]
        low = lax.ppermute(
            lax.slice_in_dim(block, block.shape[dim] - width, None, axis=dim), axis, forward
        )
        high = lax.ppermute(lax.slice_in_dim(block, 0, width, axis=dim), axis, backward)
        block = jnp.concatenate([low, block, high], axis=dim)
    return block


def convolve(values, tile_cols, tile_counts, adjacency, myself):
    window = with_halo(values, (("nodes", 0),), values.shape[0])
    tile_size = adjacency.shape[2]
    per_device = tile_cols.shape[0]
    window_tiles = window.reshape(-1, tile_size, window.shape[1])
    offsets = tile_cols - (myself - 1) * per_device
    picked = window_tiles[offsets]
    live = jnp.arange(tile_cols.shape[1], dtype=jnp.int32)[None, :] < tile_counts[:, None]
    weights = jnp.where(live[:, :, None, None], adjacency, jnp.zeros((), adjacency.dtype))
    result = jnp.einsum("tkij,tkjf->tif", weights, picked, preferred_element_type=jnp.float32)
    return result.reshape(values.shape[0], values.shape[1])


def distinct_slots(owner_hot, lid_hot, clusters_here):
    contract_rows = (((0,), (0,)), ((), ()))
    presence = lax.dot_general(owner_hot, lid_hot, contract_rows, preferred_element_type=jnp.float32)
    named = (presence > 0).astype(jnp.bfloat16)
    lanes = jnp.arange(clusters_here, dtype=jnp.int32)
    before = (lanes[:, None] < lanes[None, :]).astype(jnp.bfloat16)
    rank = jnp.dot(named, before, preferred_element_type=jnp.float32)
    return presence, rank


def local(features, cluster_ids, tile_cols, tile_counts, adjacency, w_first, w_second):
    device_count = lax.axis_size("nodes")
    myself = lax.axis_index("nodes")
    fine_rows, width = features.shape
    clusters_here = adjacency.shape[0] * adjacency.shape[2]
    owners = cluster_ids // clusters_here
    lids = cluster_ids - owners * clusters_here
    remote = owners != myself
    peers = jnp.arange(device_count, dtype=jnp.int32)
    here = jnp.arange(clusters_here, dtype=jnp.int32)
    owner_hot = (owners[:, None] == peers[None, :]).astype(jnp.bfloat16)
    lid_hot = (lids[:, None] == here[None, :]).astype(jnp.bfloat16)
    presence, rank = distinct_slots(owner_hot, lid_hot, clusters_here)

    named = (presence > 0) & (peers != myself)[:, None]
    slot_counts = []
    slot_ids = []
    for k in range(DCAP):
        chosen = named & (rank == k)
        slot_counts.append(jnp.sum(jnp.where(chosen, presence, 0.0), axis=1))
        found = jnp.sum(jnp.where(chosen, here[None, :], 0), axis=1)
        slot_ids.append(jnp.where(jnp.any(chosen, axis=1), found, clusters_here))
    slot_counts = jnp.stack(slot_counts, axis=1)
    slot_ids = jnp.stack(slot_ids, axis=1)
    split = jnp.concatenate([slot_ids // 32, slot_ids % 32], axis=1).astype(jnp.bfloat16)
    parts = jnp.dot(owner_hot, split, preferred_element_type=jnp.float32).astype(jnp.int32)
    lows = parts[:, :DCAP] * 32 + parts[:, DCAP:]
    slot = jnp.sum((lids[:, None] >= lows[:, 1:]).astype(jnp.int32), axis=1)
    remote_slots = device_count * DCAP
    slot_column = jnp.where(remote, owners * DCAP + slot, -1)
    slot_range = jnp.arange(remote_slots, dtype=jnp.int32)
    remote_hot = (slot_column[:, None] == slot_range[None, :]).astype(jnp.bfloat16)
    local_hot = jnp.where(remote[:, None], jnp.zeros((), jnp.bfloat16), lid_hot)
    contract_rows = (((0,), (0,)), ((), ()))
    remote_sums = lax.dot_general(
        remote_hot, features, contract_rows, preferred_element_type=jnp.float32
    )

    meta = jnp.concatenate(
        [slot_counts, jnp.where(slot_ids < clusters_here, slot_ids, 0).astype(jnp.float32),
         jnp.zeros((device_count, 128 - 2 * DCAP), jnp.float32)],
        axis=1,
    )
    payload = jnp.concatenate([remote_sums.reshape(device_count, DCAP * width), meta], axis=1)
    got = lax.all_to_all(
        payload.reshape(device_count, 1, -1), "nodes", split_axis=0, concat_axis=0, tiled=True
    ).reshape(device_count, -1)
    got_sums = got[:, : DCAP * width].reshape(remote_slots, width)
    got_counts = got[:, DCAP * width : DCAP * width + DCAP].reshape(remote_slots)
    got_ids = got[:, DCAP * width + DCAP : DCAP * width + 2 * DCAP].reshape(remote_slots).astype(jnp.int32)
    local_sums = lax.dot_general(
        local_hot, features, contract_rows, preferred_element_type=jnp.float32
    )
    local_counts = lax.dynamic_index_in_dim(presence, myself, axis=0, keepdims=False)
    got_hot = (got_ids[:, None] == here[None, :]).astype(jnp.float32)
    sums_all = local_sums + lax.dot_general(
        got_hot, got_sums, contract_rows,
        precision=lax.Precision.HIGHEST, preferred_element_type=jnp.float32,
    )
    counts_all = local_counts + jnp.sum(got_hot * got_counts[:, None], axis=0)
    pooled = (sums_all / jnp.sqrt(counts_all + 1.0)[:, None]).astype(jnp.bfloat16)
    first_proj = jnp.dot(pooled, w_first, preferred_element_type=jnp.float32).astype(jnp.bfloat16)
    hidden = jnp.maximum(
        convolve(first_proj, tile_cols, tile_counts, adjacency, myself), 0.0
    ).astype(jnp.bfloat16)
    second_proj = jnp.dot(hidden, w_second, preferred_element_type=jnp.float32).astype(jnp.bfloat16)
    coarse = convolve(second_proj, tile_cols, tile_counts, adjacency, myself).astype(jnp.bfloat16)
    answers = jnp.dot(
        got_hot.astype(jnp.bfloat16), coarse, preferred_element_type=jnp.float32
    ).astype(jnp.bfloat16)
    returned = lax.all_to_all(
        answers.reshape(device_count, DCAP, width), "nodes", split_axis=0, concat_axis=0, tiled=True
    ).reshape(remote_slots, width)
    first = add_rows(jnp.where(remote, -1, lids), features, coarse)
    return add_rows(slot_column, first, returned)


def solution(mesh):
    placed = (
        P("nodes", None),
        P("nodes"),
        P("nodes", None),
        P("nodes"),
        P("nodes", None, None, None),
        P(),
        P(),
    )
    return jax.shard_map(
        local, mesh=mesh, in_specs=placed, out_specs=P("nodes", None), check_vma=False
    )
```

```python
import jax
import jax.numpy as jnp
from jax import lax
from jax.sharding import PartitionSpec as P

DCAP = 4


def with_halo(block, sides, width):
    for axis, dim in sides:
        count = lax.axis_size(axis)
        forward = [(i, i + 1) for i in range(count - 1)]
        backward = [(target, source) for source, target in forward]
        low = lax.ppermute(
            lax.slice_in_dim(block, block.shape[dim] - width, None, axis=dim), axis, forward
        )
        high = lax.ppermute(lax.slice_in_dim(block, 0, width, axis=dim), axis, backward)
        block = jnp.concatenate([low, block, high], axis=dim)
    return block


def convolve(values, tile_cols, tile_counts, adjacency, myself):
    count = lax.axis_size("nodes")
    forward = [(i, i + 1) for i in range(count - 1)]
    backward = [(target, source) for source, target in forward]
    low = lax.ppermute(values, "nodes", forward)
    high = lax.ppermute(values, "nodes", backward)
    tile_size = adjacency.shape[2]
    per_device = tile_cols.shape[0]
    offsets = tile_cols - myself * per_device
    live = jnp.arange(tile_cols.shape[1], dtype=jnp.int32)[None, :] < tile_counts[:, None]

    def term(block, shift):
        tiles = block.reshape(-1, tile_size, block.shape[1])
        place = offsets - shift
        inside = live & (place >= 0) & (place < per_device)
        picked = tiles[jnp.clip(place, 0, per_device - 1)]
        weights = jnp.where(inside[:, :, None, None], adjacency, jnp.zeros((), adjacency.dtype))
        return jnp.einsum("tkij,tkjf->tif", weights, picked, preferred_element_type=jnp.float32)

    result = term(values, 0) + term(low, -per_device) + term(high, per_device)
    return result.reshape(values.shape[0], values.shape[1])


def distinct_slots(owner_hot, lid_hot, clusters_here):
    contract_rows = (((0,), (0,)), ((), ()))
    presence = lax.dot_general(owner_hot, lid_hot, contract_rows, preferred_element_type=jnp.float32)
    named = (presence > 0).astype(jnp.bfloat16)
    lanes = jnp.arange(clusters_here, dtype=jnp.int32)
    before = (lanes[:, None] < lanes[None, :]).astype(jnp.bfloat16)
    rank = jnp.dot(named, before, preferred_element_type=jnp.float32)
    per_owner = jnp.dot(lid_hot, rank.T.astype(jnp.bfloat16), preferred_element_type=jnp.float32)
    slot = jnp.sum(per_owner * owner_hot.astype(jnp.float32), axis=1).astype(jnp.int32)
    return presence, rank, slot


def local(features, cluster_ids, tile_cols, tile_counts, adjacency, w_first, w_second):
    device_count = lax.axis_size("nodes")
    myself = lax.axis_index("nodes")
    fine_rows, width = features.shape
    clusters_here = adjacency.shape[0] * adjacency.shape[2]
    owners = cluster_ids // clusters_here
    lids = cluster_ids - owners * clusters_here
    remote = owners != myself
    peers = jnp.arange(device_count, dtype=jnp.int32)
    here = jnp.arange(clusters_here, dtype=jnp.int32)
    owner_hot = (owners[:, None] == peers[None, :]).astype(jnp.bfloat16)
    lid_hot = (lids[:, None] == here[None, :]).astype(jnp.bfloat16)
    presence, rank, slot = distinct_slots(owner_hot, lid_hot, clusters_here)
    remote_slots = device_count * DCAP
    slot_column = jnp.where(remote, owners * DCAP + slot, -1)
    slot_range = jnp.arange(remote_slots, dtype=jnp.int32)
    remote_hot = (slot_column[:, None] == slot_range[None, :]).astype(jnp.bfloat16)
    local_hot = jnp.where(remote[:, None], jnp.zeros((), jnp.bfloat16), lid_hot)
    contract_rows = (((0,), (0,)), ((), ()))
    remote_sums = lax.dot_general(
        remote_hot, features, contract_rows, preferred_element_type=jnp.float32
    )

    named = (presence > 0) & (peers != myself)[:, None]
    slot_counts = []
    slot_ids = []
    for k in range(DCAP):
        chosen = named & (rank == k)
        slot_counts.append(jnp.sum(jnp.where(chosen, presence, 0.0), axis=1))
        slot_ids.append(jnp.sum(jnp.where(chosen, here[None, :], 0), axis=1))
    slot_counts = jnp.stack(slot_counts, axis=1)
    slot_ids = jnp.stack(slot_ids, axis=1).astype(jnp.float32)
    meta = jnp.concatenate(
        [slot_counts, slot_ids, jnp.zeros((device_count, 128 - 2 * DCAP), jnp.float32)], axis=1
    )
    payload = jnp.concatenate([remote_sums.reshape(device_count, DCAP * width), meta], axis=1)
    got = lax.all_to_all(
        payload.reshape(device_count, 1, -1), "nodes", split_axis=0, concat_axis=0, tiled=True
    ).reshape(device_count, -1)
    got_sums = got[:, : DCAP * width].reshape(remote_slots, width)
    got_counts = got[:, DCAP * width : DCAP * width + DCAP].reshape(remote_slots)
    got_ids = got[:, DCAP * width + DCAP : DCAP * width + 2 * DCAP].reshape(remote_slots).astype(jnp.int32)
    local_sums = lax.dot_general(
        local_hot, features, contract_rows, preferred_element_type=jnp.float32
    )
    local_counts = lax.dynamic_index_in_dim(presence, myself, axis=0, keepdims=False)
    got_hot = (got_ids[:, None] == here[None, :]).astype(jnp.float32)
    sums_all = local_sums + lax.dot_general(
        got_hot, got_sums, contract_rows,
        precision=lax.Precision.HIGHEST, preferred_element_type=jnp.float32,
    )
    counts_all = local_counts + jnp.sum(got_hot * got_counts[:, None], axis=0)
    pooled = (sums_all / jnp.sqrt(counts_all + 1.0)[:, None]).astype(jnp.bfloat16)
    first_proj = jnp.dot(pooled, w_first, preferred_element_type=jnp.float32).astype(jnp.bfloat16)
    hidden = jnp.maximum(
        convolve(first_proj, tile_cols, tile_counts, adjacency, myself), 0.0
    ).astype(jnp.bfloat16)
    second_proj = jnp.dot(hidden, w_second, preferred_element_type=jnp.float32).astype(jnp.bfloat16)
    coarse = convolve(second_proj, tile_cols, tile_counts, adjacency, myself).astype(jnp.bfloat16)
    answers = jnp.dot(
        got_hot.astype(jnp.bfloat16), coarse, preferred_element_type=jnp.float32
    ).astype(jnp.bfloat16)
    returned = lax.all_to_all(
        answers.reshape(device_count, DCAP, width), "nodes", split_axis=0, concat_axis=0, tiled=True
    ).reshape(remote_slots, width)
    value = (
        features.astype(jnp.float32)
        + jnp.dot(local_hot, coarse, preferred_element_type=jnp.float32)
        + jnp.dot(remote_hot, returned, preferred_element_type=jnp.float32)
    )
    return value.astype(jnp.bfloat16)


def solution(mesh):
    placed = (
        P("nodes", None),
        P("nodes"),
        P("nodes", None),
        P("nodes"),
        P("nodes", None, None, None),
        P(),
        P(),
    )
    return jax.shard_map(
        local, mesh=mesh, in_specs=placed, out_specs=P("nodes", None), check_vma=False
    )
```

```python
import jax
import jax.numpy as jnp
from jax import lax
from jax.sharding import PartitionSpec as P

DCAP = 4


def with_halo(block, sides, width):
    for axis, dim in sides:
        count = lax.axis_size(axis)
        forward = [(i, i + 1) for i in range(count - 1)]
        backward = [(target, source) for source, target in forward]
        low = lax.ppermute(
            lax.slice_in_dim(block, block.shape[dim] - width, None, axis=dim), axis, forward
        )
        high = lax.ppermute(lax.slice_in_dim(block, 0, width, axis=dim), axis, backward)
        block = jnp.concatenate([low, block, high], axis=dim)
    return block


def convolve(values, tile_cols, tile_counts, adjacency, myself):
    window = with_halo(values, (("nodes", 0),), values.shape[0])
    tile_size = adjacency.shape[2]
    per_device = tile_cols.shape[0]
    window_tiles = window.reshape(-1, tile_size, window.shape[1])
    offsets = tile_cols - (myself - 1) * per_device
    picked = window_tiles[offsets]
    live = jnp.arange(tile_cols.shape[1], dtype=jnp.int32)[None, :] < tile_counts[:, None]
    weights = jnp.where(live[:, :, None, None], adjacency, jnp.zeros((), adjacency.dtype))
    result = jnp.einsum("tkij,tkjf->tif", weights, picked, preferred_element_type=jnp.float32)
    return result.reshape(values.shape[0], values.shape[1])


def distinct_slots(owner_hot, lid_hot, clusters_here):
    contract_rows = (((0,), (0,)), ((), ()))
    presence = lax.dot_general(owner_hot, lid_hot, contract_rows, preferred_element_type=jnp.float32)
    named = (presence > 0).astype(jnp.bfloat16)
    lanes = jnp.arange(clusters_here, dtype=jnp.int32)
    before = (lanes[:, None] < lanes[None, :]).astype(jnp.bfloat16)
    rank = jnp.dot(named, before, preferred_element_type=jnp.float32)
    per_owner = jnp.dot(lid_hot, rank.T.astype(jnp.bfloat16), preferred_element_type=jnp.float32)
    slot = jnp.sum(per_owner * owner_hot.astype(jnp.float32), axis=1).astype(jnp.int32)
    return presence, rank, slot


def local(features, cluster_ids, tile_cols, tile_counts, adjacency, w_first, w_second):
    device_count = lax.axis_size("nodes")
    myself = lax.axis_index("nodes")
    fine_rows, width = features.shape
    clusters_here = adjacency.shape[0] * adjacency.shape[2]
    owners = cluster_ids // clusters_here
    lids = cluster_ids - owners * clusters_here
    remote = owners != myself
    peers = jnp.arange(device_count, dtype=jnp.int32)
    here = jnp.arange(clusters_here, dtype=jnp.int32)
    owner_hot = (owners[:, None] == peers[None, :]).astype(jnp.bfloat16)
    lid_hot = (lids[:, None] == here[None, :]).astype(jnp.bfloat16)
    presence, rank, slot = distinct_slots(owner_hot, lid_hot, clusters_here)
    remote_slots = device_count * DCAP
    slot_column = jnp.where(remote, slot * device_count + owners, -1)
    slot_range = jnp.arange(remote_slots, dtype=jnp.int32)
    remote_hot = (slot_column[:, None] == slot_range[None, :]).astype(jnp.bfloat16)
    local_hot = jnp.where(remote[:, None], jnp.zeros((), jnp.bfloat16), lid_hot)
    contract_rows = (((0,), (0,)), ((), ()))
    remote_sums = lax.dot_general(
        remote_hot, features, contract_rows, preferred_element_type=jnp.float32
    )

    named = (presence > 0) & (peers != myself)[:, None]
    slot_counts = []
    slot_ids = []
    for k in range(DCAP):
        chosen = named & (rank == k)
        slot_counts.append(jnp.sum(jnp.where(chosen, presence, 0.0), axis=1))
        slot_ids.append(jnp.sum(jnp.where(chosen, here[None, :], 0), axis=1))
    slot_counts = jnp.stack(slot_counts, axis=1)
    slot_ids = jnp.stack(slot_ids, axis=1).astype(jnp.float32)
    meta = jnp.concatenate(
        [slot_counts, slot_ids, jnp.zeros((device_count, 128 - 2 * DCAP), jnp.float32)], axis=1
    )
    payload = jnp.concatenate(
        [remote_sums[k * device_count:(k + 1) * device_count] for k in range(DCAP)] + [meta], axis=1
    )
    got = lax.all_to_all(
        payload.reshape(device_count, 1, -1), "nodes", split_axis=0, concat_axis=0, tiled=True
    ).reshape(device_count, -1)
    got_sums = jnp.concatenate([got[:, k * width:(k + 1) * width] for k in range(DCAP)], axis=0)
    got_counts = got[:, DCAP * width : DCAP * width + DCAP].T.reshape(remote_slots)
    got_ids = got[:, DCAP * width + DCAP : DCAP * width + 2 * DCAP].T.reshape(remote_slots).astype(jnp.int32)
    local_sums = lax.dot_general(
        local_hot, features, contract_rows, preferred_element_type=jnp.float32
    )
    local_counts = lax.dynamic_index_in_dim(presence, myself, axis=0, keepdims=False)
    got_hot = (got_ids[:, None] == here[None, :]).astype(jnp.float32)
    sums_all = local_sums + lax.dot_general(
        got_hot, got_sums, contract_rows,
        precision=lax.Precision.HIGHEST, preferred_element_type=jnp.float32,
    )
    counts_all = local_counts + jnp.sum(got_hot * got_counts[:, None], axis=0)
    pooled = (sums_all / jnp.sqrt(counts_all + 1.0)[:, None]).astype(jnp.bfloat16)
    first_proj = jnp.dot(pooled, w_first, preferred_element_type=jnp.float32).astype(jnp.bfloat16)
    hidden = jnp.maximum(
        convolve(first_proj, tile_cols, tile_counts, adjacency, myself), 0.0
    ).astype(jnp.bfloat16)
    second_proj = jnp.dot(hidden, w_second, preferred_element_type=jnp.float32).astype(jnp.bfloat16)
    coarse = convolve(second_proj, tile_cols, tile_counts, adjacency, myself).astype(jnp.bfloat16)
    answers = jnp.dot(
        got_hot.astype(jnp.bfloat16), coarse, preferred_element_type=jnp.float32
    ).astype(jnp.bfloat16)
    back = jnp.concatenate(
        [answers[k * device_count:(k + 1) * device_count] for k in range(DCAP)], axis=1
    )
    returned = lax.all_to_all(
        back.reshape(device_count, 1, -1), "nodes", split_axis=0, concat_axis=0, tiled=True
    ).reshape(device_count, -1)
    returned = jnp.concatenate([returned[:, k * width:(k + 1) * width] for k in range(DCAP)], axis=0)
    value = (
        features.astype(jnp.float32)
        + jnp.dot(local_hot, coarse, preferred_element_type=jnp.float32)
        + jnp.dot(remote_hot, returned, preferred_element_type=jnp.float32)
    )
    return value.astype(jnp.bfloat16)


def solution(mesh):
    placed = (
        P("nodes", None),
        P("nodes"),
        P("nodes", None),
        P("nodes"),
        P("nodes", None, None, None),
        P(),
        P(),
    )
    return jax.shard_map(
        local, mesh=mesh, in_specs=placed, out_specs=P("nodes", None), check_vma=False
    )
```

```python
import jax
import jax.numpy as jnp
from jax import lax
from jax.sharding import PartitionSpec as P

DCAP = 4


def with_halo(block, sides, width):
    for axis, dim in sides:
        count = lax.axis_size(axis)
        forward = [(i, i + 1) for i in range(count - 1)]
        backward = [(target, source) for source, target in forward]
        low = lax.ppermute(
            lax.slice_in_dim(block, block.shape[dim] - width, None, axis=dim), axis, forward
        )
        high = lax.ppermute(lax.slice_in_dim(block, 0, width, axis=dim), axis, backward)
        block = jnp.concatenate([low, block, high], axis=dim)
    return block


def convolve(values, tile_cols, tile_counts, adjacency, myself):
    window = with_halo(values, (("nodes", 0),), values.shape[0])
    tile_size = adjacency.shape[2]
    per_device = tile_cols.shape[0]
    window_tiles = window.reshape(-1, tile_size, window.shape[1])
    offsets = tile_cols - (myself - 1) * per_device
    picked = window_tiles[offsets]
    live = jnp.arange(tile_cols.shape[1], dtype=jnp.int32)[None, :] < tile_counts[:, None]
    weights = jnp.where(live[:, :, None, None], adjacency, jnp.zeros((), adjacency.dtype))
    result = jnp.einsum("tkij,tkjf->tif", weights, picked, preferred_element_type=jnp.float32)
    return result.reshape(values.shape[0], values.shape[1])


def distinct_slots(owner_hot, lid_hot, clusters_here):
    contract_rows = (((0,), (0,)), ((), ()))
    presence = lax.dot_general(owner_hot, lid_hot, contract_rows, preferred_element_type=jnp.float32)
    named = (presence > 0).astype(jnp.bfloat16)
    lanes = jnp.arange(clusters_here, dtype=jnp.int32)
    before = (lanes[:, None] < lanes[None, :]).astype(jnp.bfloat16)
    rank = jnp.dot(named, before, preferred_element_type=jnp.float32)
    return presence, rank


def local(features, cluster_ids, tile_cols, tile_counts, adjacency, w_first, w_second):
    device_count = lax.axis_size("nodes")
    myself = lax.axis_index("nodes")
    fine_rows, width = features.shape
    clusters_here = adjacency.shape[0] * adjacency.shape[2]
    owners = cluster_ids // clusters_here
    lids = cluster_ids - owners * clusters_here
    remote = owners != myself
    peers = jnp.arange(device_count, dtype=jnp.int32)
    here = jnp.arange(clusters_here, dtype=jnp.int32)
    owner_hot = (owners[:, None] == peers[None, :]).astype(jnp.bfloat16)
    lid_hot = (lids[:, None] == here[None, :]).astype(jnp.bfloat16)
    presence, rank = distinct_slots(owner_hot, lid_hot, clusters_here)

    named = (presence > 0) & (peers != myself)[:, None]
    slot_counts = []
    slot_ids = []
    for k in range(DCAP):
        chosen = named & (rank == k)
        slot_counts.append(jnp.sum(jnp.where(chosen, presence, 0.0), axis=1))
        found = jnp.sum(jnp.where(chosen, here[None, :], 0), axis=1)
        slot_ids.append(jnp.where(jnp.any(chosen, axis=1), found, clusters_here))
    slot_counts = jnp.stack(slot_counts, axis=1)
    slot_ids = jnp.stack(slot_ids, axis=1)
    split = jnp.concatenate([slot_ids // 32, slot_ids % 32], axis=1).astype(jnp.bfloat16)
    parts = jnp.dot(owner_hot, split, preferred_element_type=jnp.float32).astype(jnp.int32)
    lows = parts[:, :DCAP] * 32 + parts[:, DCAP:]
    slot = jnp.sum((lids[:, None] >= lows[:, 1:]).astype(jnp.int32), axis=1)
    remote_slots = device_count * DCAP
    slot_column = jnp.where(remote, slot * device_count + owners, -1)
    slot_range = jnp.arange(remote_slots, dtype=jnp.int32)
    remote_hot = (slot_column[:, None] == slot_range[None, :]).astype(jnp.bfloat16)
    local_hot = jnp.where(remote[:, None], jnp.zeros((), jnp.bfloat16), lid_hot)
    contract_rows = (((0,), (0,)), ((), ()))
    remote_sums = lax.dot_general(
        remote_hot, features, contract_rows, preferred_element_type=jnp.float32
    )

    meta = jnp.concatenate(
        [slot_counts, jnp.where(slot_ids < clusters_here, slot_ids, 0).astype(jnp.float32),
         jnp.zeros((device_count, 128 - 2 * DCAP), jnp.float32)],
        axis=1,
    )
    payload = jnp.concatenate(
        [remote_sums[k * device_count:(k + 1) * device_count] for k in range(DCAP)] + [meta], axis=1
    )
    got = lax.all_to_all(
        payload.reshape(device_count, 1, -1), "nodes", split_axis=0, concat_axis=0, tiled=True
    ).reshape(device_count, -1)
    got_sums = jnp.concatenate([got[:, k * width:(k + 1) * width] for k in range(DCAP)], axis=0)
    got_counts = got[:, DCAP * width : DCAP * width + DCAP].T.reshape(remote_slots)
    got_ids = got[:, DCAP * width + DCAP : DCAP * width + 2 * DCAP].T.reshape(remote_slots).astype(jnp.int32)
    local_sums = lax.dot_general(
        local_hot, features, contract_rows, preferred_element_type=jnp.float32
    )
    local_counts = lax.dynamic_index_in_dim(presence, myself, axis=0, keepdims=False)
    got_hot = (got_ids[:, None] == here[None, :]).astype(jnp.float32)
    sums_all = local_sums + lax.dot_general(
        got_hot, got_sums, contract_rows,
        precision=lax.Precision.HIGHEST, preferred_element_type=jnp.float32,
    )
    counts_all = local_counts + jnp.sum(got_hot * got_counts[:, None], axis=0)
    pooled = (sums_all / jnp.sqrt(counts_all + 1.0)[:, None]).astype(jnp.bfloat16)
    first_proj = jnp.dot(pooled, w_first, preferred_element_type=jnp.float32).astype(jnp.bfloat16)
    hidden = jnp.maximum(
        convolve(first_proj, tile_cols, tile_counts, adjacency, myself), 0.0
    ).astype(jnp.bfloat16)
    second_proj = jnp.dot(hidden, w_second, preferred_element_type=jnp.float32).astype(jnp.bfloat16)
    coarse = convolve(second_proj, tile_cols, tile_counts, adjacency, myself).astype(jnp.bfloat16)
    answers = jnp.dot(
        got_hot.astype(jnp.bfloat16), coarse, preferred_element_type=jnp.float32
    ).astype(jnp.bfloat16)
    back = jnp.concatenate(
        [answers[k * device_count:(k + 1) * device_count] for k in range(DCAP)], axis=1
    )
    returned = lax.all_to_all(
        back.reshape(device_count, 1, -1), "nodes", split_axis=0, concat_axis=0, tiled=True
    ).reshape(device_count, -1)
    returned = jnp.concatenate([returned[:, k * width:(k + 1) * width] for k in range(DCAP)], axis=0)
    value = (
        features.astype(jnp.float32)
        + jnp.dot(local_hot, coarse, preferred_element_type=jnp.float32)
        + jnp.dot(remote_hot, returned, preferred_element_type=jnp.float32)
    )
    return value.astype(jnp.bfloat16)


def solution(mesh):
    placed = (
        P("nodes", None),
        P("nodes"),
        P("nodes", None),
        P("nodes"),
        P("nodes", None, None, None),
        P(),
        P(),
    )
    return jax.shard_map(
        local, mesh=mesh, in_specs=placed, out_specs=P("nodes", None), check_vma=False
    )
```

```python
import jax
import jax.numpy as jnp
from jax import lax
from jax.sharding import PartitionSpec as P

DCAP = 4


def with_halo(block, sides, width):
    for axis, dim in sides:
        count = lax.axis_size(axis)
        forward = [(i, i + 1) for i in range(count - 1)]
        backward = [(target, source) for source, target in forward]
        low = lax.ppermute(
            lax.slice_in_dim(block, block.shape[dim] - width, None, axis=dim), axis, forward
        )
        high = lax.ppermute(lax.slice_in_dim(block, 0, width, axis=dim), axis, backward)
        block = jnp.concatenate([low, block, high], axis=dim)
    return block


def convolve(values, tile_cols, tile_counts, adjacency, myself):
    window = with_halo(values, (("nodes", 0),), values.shape[0])
    tile_size = adjacency.shape[2]
    per_device = tile_cols.shape[0]
    window_tiles = window.reshape(-1, tile_size, window.shape[1])
    offsets = tile_cols - (myself - 1) * per_device
    picked = window_tiles[offsets]
    live = jnp.arange(tile_cols.shape[1], dtype=jnp.int32)[None, :] < tile_counts[:, None]
    weights = jnp.where(live[:, :, None, None], adjacency, jnp.zeros((), adjacency.dtype))
    result = jnp.einsum("tkij,tkjf->tif", weights, picked, preferred_element_type=jnp.float32)
    return result.reshape(values.shape[0], values.shape[1])


def distinct_slots(owner_hot, lid_hot, clusters_here):
    contract_rows = (((0,), (0,)), ((), ()))
    presence = lax.dot_general(owner_hot, lid_hot, contract_rows, preferred_element_type=jnp.float32)
    named = (presence > 0).astype(jnp.bfloat16)
    lanes = jnp.arange(clusters_here, dtype=jnp.int32)
    before = (lanes[:, None] < lanes[None, :]).astype(jnp.bfloat16)
    rank = jnp.dot(named, before, preferred_element_type=jnp.float32)
    per_owner = jnp.dot(lid_hot, rank.T.astype(jnp.bfloat16), preferred_element_type=jnp.float32)
    slot = jnp.sum(per_owner * owner_hot.astype(jnp.float32), axis=1).astype(jnp.int32)
    return presence, rank, slot


def local(features, cluster_ids, tile_cols, tile_counts, adjacency, w_first, w_second):
    device_count = lax.axis_size("nodes")
    myself = lax.axis_index("nodes")
    fine_rows, width = features.shape
    clusters_here = adjacency.shape[0] * adjacency.shape[2]
    owners = cluster_ids // clusters_here
    lids = cluster_ids - owners * clusters_here
    remote = owners != myself
    peers = jnp.arange(device_count, dtype=jnp.int32)
    here = jnp.arange(clusters_here, dtype=jnp.int32)
    owner_hot = (owners[:, None] == peers[None, :]).astype(jnp.bfloat16)
    lid_hot = (lids[:, None] == here[None, :]).astype(jnp.bfloat16)
    presence, rank, slot = distinct_slots(owner_hot, lid_hot, clusters_here)
    remote_slots = device_count * DCAP
    slot_column = jnp.where(remote, slot * device_count + owners, -1)
    slot_range = jnp.arange(remote_slots, dtype=jnp.int32)
    remote_hot = (slot_column[:, None] == slot_range[None, :]).astype(jnp.bfloat16)
    local_hot = jnp.where(remote[:, None], jnp.zeros((), jnp.bfloat16), lid_hot)
    contract_rows = (((0,), (0,)), ((), ()))
    remote_sums = lax.dot_general(
        remote_hot, features, contract_rows, preferred_element_type=jnp.float32
    )

    named = (presence > 0) & (peers != myself)[:, None]
    slot_counts = []
    slot_ids = []
    for k in range(DCAP):
        chosen = named & (rank == k)
        slot_counts.append(jnp.sum(jnp.where(chosen, presence, 0.0), axis=1))
        slot_ids.append(jnp.sum(jnp.where(chosen, here[None, :], 0), axis=1))
    slot_counts = jnp.stack(slot_counts, axis=1)
    slot_ids = jnp.stack(slot_ids, axis=1).astype(jnp.float32)
    meta = jnp.concatenate(
        [slot_counts, slot_ids, jnp.zeros((device_count, 128 - 2 * DCAP), jnp.float32)], axis=1
    )
    payload = jnp.concatenate(
        [remote_sums[k * device_count:(k + 1) * device_count] for k in range(DCAP)] + [meta], axis=1
    )
    got = lax.all_to_all(
        payload.reshape(device_count, 1, -1), "nodes", split_axis=0, concat_axis=0, tiled=True
    ).reshape(device_count, -1)
    got_sums = jnp.concatenate([got[:, k * width:(k + 1) * width] for k in range(DCAP)], axis=0)
    got_counts = got[:, DCAP * width : DCAP * width + DCAP].T.reshape(remote_slots)
    got_ids = got[:, DCAP * width + DCAP : DCAP * width + 2 * DCAP].T.reshape(remote_slots).astype(jnp.int32)
    local_sums = lax.dot_general(
        local_hot, features, contract_rows, preferred_element_type=jnp.float32
    )
    local_counts = lax.dynamic_index_in_dim(presence, myself, axis=0, keepdims=False)
    got_hot = (got_ids[:, None] == here[None, :]).astype(jnp.bfloat16)
    got_high = got_sums.astype(jnp.bfloat16)
    got_low = (got_sums - got_high.astype(jnp.float32)).astype(jnp.bfloat16)
    sums_all = (
        local_sums
        + lax.dot_general(got_hot, got_high, contract_rows, preferred_element_type=jnp.float32)
        + lax.dot_general(got_hot, got_low, contract_rows, preferred_element_type=jnp.float32)
    )
    counts_all = local_counts + jnp.sum(got_hot.astype(jnp.float32) * got_counts[:, None], axis=0)
    pooled = (sums_all / jnp.sqrt(counts_all + 1.0)[:, None]).astype(jnp.bfloat16)
    first_proj = jnp.dot(pooled, w_first, preferred_element_type=jnp.float32).astype(jnp.bfloat16)
    hidden = jnp.maximum(
        convolve(first_proj, tile_cols, tile_counts, adjacency, myself), 0.0
    ).astype(jnp.bfloat16)
    second_proj = jnp.dot(hidden, w_second, preferred_element_type=jnp.float32).astype(jnp.bfloat16)
    coarse = convolve(second_proj, tile_cols, tile_counts, adjacency, myself).astype(jnp.bfloat16)
    answers = jnp.dot(
        got_hot, coarse, preferred_element_type=jnp.float32
    ).astype(jnp.bfloat16)
    back = jnp.concatenate(
        [answers[k * device_count:(k + 1) * device_count] for k in range(DCAP)], axis=1
    )
    returned = lax.all_to_all(
        back.reshape(device_count, 1, -1), "nodes", split_axis=0, concat_axis=0, tiled=True
    ).reshape(device_count, -1)
    returned = jnp.concatenate([returned[:, k * width:(k + 1) * width] for k in range(DCAP)], axis=0)
    value = (
        features.astype(jnp.float32)
        + jnp.dot(local_hot, coarse, preferred_element_type=jnp.float32)
        + jnp.dot(remote_hot, returned, preferred_element_type=jnp.float32)
    )
    return value.astype(jnp.bfloat16)


def solution(mesh):
    placed = (
        P("nodes", None),
        P("nodes"),
        P("nodes", None),
        P("nodes"),
        P("nodes", None, None, None),
        P(),
        P(),
    )
    return jax.shard_map(
        local, mesh=mesh, in_specs=placed, out_specs=P("nodes", None), check_vma=False
    )
```
